1024 devices in a mesh: seq: 128 (over y, z), head: 8 (over x, core).
Axes of the slice: x: 4, y: 8, z: 16, core: 2. Of those that a mesh axis runs over, the one named last changes fastest.
Arguments:
- queries: bfloat16 [32768, 3072], P('seq', 'head'), may hold values from -8 to 8
- key_states: bfloat16 [32768, 3072], P('seq', 'head'), may hold values from -8 to 8
- value_states: bfloat16 [32768, 3072], P('seq', 'head'), may hold values from -12 to 12
- level_offsets: int32 [3, 24], P(None, 'head'), may hold values from 0 to 31
- out_weight: bfloat16 [3072, 5120], P(None, 'head'), may hold values from -0.109375 to 0.109375
Outputs:
- layer_output: bfloat16 [32768, 5120], P('seq', 'head')
The draws below stay inside these ranges and needn't reach their ends.
All inputs are finite; a program needn't handle non-finite values.
Results may differ from the reference program's by a relative error of at most 0.0057.
Values may be sent and summed in bfloat16 or wider, within the bound.
No kernel may reach another device: no remote copies, remote signals or barrier semaphores. Data moves between devices by JAX's collectives and lax.ppermute only.
A program may use at most 32 MiB of HBM per device.

```python
import jax
import jax.numpy as jnp
from jax import lax

D = 5120
HD = 128
HEADS = 24
LEVELS = 3
RATE_MID = 8
RATE_TOP = 32
SEG_ROWS = 1024
TOK_DEV = 256
TOKENS = 32768
N_SEQ = 128


def paired_states(key):
    columns = HEADS * HD
    query_rows = 1.3 * jax.random.normal(jax.random.fold_in(key, 11), (TOKENS, columns), jnp.float32)
    key_rows = 1.3 * jax.random.normal(jax.random.fold_in(key, 12), (TOKENS, columns), jnp.float32)
    return (jnp.clip(query_rows, -8.0, 8.0), jnp.clip(key_rows, -8.0, 8.0))


def draw_queries(key, part):
    return paired_states(key)[0].astype(jnp.bfloat16)


def draw_key_states(key, part):
    return paired_states(key)[1].astype(jnp.bfloat16)


def set_ends(array, key, low, top_value):
    place = [jax.random.randint(jax.random.fold_in(key, axis), (), 0, length) for axis, length in enumerate(array.shape)]
    widest = array.shape.index(max(array.shape))
    beside = place[:widest] + [(place[widest] + 1) % array.shape[widest]] + place[widest + 1:]
    return array.at[tuple(place)].set(low).at[tuple(beside)].set(top_value)


def steps_of(rng, extent, split, low, top_value):
    factor_of, own = 1.0, jax.random.fold_in(rng, 6)
    for axis_at, parts in split:
        heights = jnp.exp(jax.random.uniform(jax.random.fold_in(own, axis_at), (parts,), jnp.float32, low / len(split), top_value / len(split)))
        factor_of = factor_of * jnp.repeat(heights, extent[axis_at] // parts).reshape([-1 if axis == axis_at else 1 for axis in range(len(extent))])
    return factor_of


def noise(stream_key, extent, width, reach, shards=(), kind=jnp.bfloat16):
    values = width * jax.random.normal(stream_key, extent, jnp.float32)
    if shards:
        values = values * steps_of(stream_key, extent, shards, -0.22, 0.18)
    return jnp.clip(values, -reach, reach).astype(kind)


def setup_inputs(seed: int = 0) -> dict:
    key_of = jax.random.split(jax.random.key(seed), 6)
    queries = draw_queries(jax.random.fold_in(key_of[5], 71), 0)
    key_states = draw_key_states(jax.random.fold_in(key_of[5], 71), 0)
    value_states = noise(key_of[2], (TOKENS, HEADS * HD), 2.0, 12.0, ((0, 128), (1, 8)))
    level_offsets = set_ends(jax.random.randint(key_of[3], (LEVELS, HEADS), 0, RATE_TOP), jax.random.fold_in(key_of[3], 1), 0, RATE_TOP - 1).astype(jnp.int32)
    out_weight = noise(key_of[4], (HEADS * HD, D), (HEADS * HD) ** -0.5, 0.109375, ((1, 8),))
    return {"queries": queries, "key_states": key_states, "value_states": value_states, "level_offsets": level_offsets, "out_weight": out_weight}


NEG_FILL = -1e30


def spread_back(level_out, level_lse, offset, spacing):
    picked = jnp.arange(spacing, dtype=jnp.int32) == offset
    full_out = (level_out[:, None, :] * picked.astype(level_out.dtype)[None, :, None]).reshape(-1, level_out.shape[1])
    full_lse = jnp.where(picked[None, :], level_lse[:, None], NEG_FILL).reshape(-1)
    return full_out, full_lse


def head_result(inputs):
    query_head, key_head, value_head, offset_head = inputs
    scale_factor = HD ** -0.5
    level_outs = []
    level_lses = []
    for level_no, spacing in enumerate((1, RATE_MID, RATE_TOP)):
        span_devices = min(SEG_ROWS * spacing // TOK_DEV, N_SEQ)
        seg_rows = span_devices * TOK_DEV // spacing
        offset = (offset_head[level_no] % spacing).astype(jnp.int32)

        def pick_level(full_rows):
            grouped = full_rows.reshape(TOKENS // spacing, spacing, HD)
            chosen = lax.dynamic_index_in_dim(grouped, offset, 1, keepdims=False)
            return chosen.reshape(-1, seg_rows, HD).astype(jnp.float32)

        query_rows = pick_level(query_head)
        key_rows = pick_level(key_head)
        value_rows = pick_level(value_head)
        scores = jnp.einsum("sqd,skd->sqk", query_rows, key_rows, precision=lax.Precision.HIGHEST) * scale_factor
        causal = jnp.tril(jnp.ones((seg_rows, seg_rows), dtype=bool))
        scores = jnp.where(causal[None], scores, NEG_FILL)
        highest = jnp.max(scores, axis=2, keepdims=True)
        weights = jnp.exp(scores - highest)
        totals = jnp.sum(weights, axis=2, keepdims=True)
        shares = (weights / totals).astype(jnp.bfloat16).astype(jnp.float32)
        level_out = jnp.einsum("sqk,skd->sqd", shares, value_rows, precision=lax.Precision.HIGHEST).reshape(-1, HD)
        level_lse = (highest + jnp.log(totals)).reshape(-1)
        full_out, full_lse = spread_back(level_out, level_lse, offset, spacing)
        level_outs.append(full_out)
        level_lses.append(full_lse)
    lse_stack = jnp.stack(level_lses)
    level_top = jnp.max(lse_stack, axis=0)
    level_weights = jnp.exp(lse_stack - level_top[None])
    mixed_heads = jnp.sum(level_weights[:, :, None] * jnp.stack(level_outs), axis=0) / jnp.sum(level_weights, axis=0)[:, None]
    return mixed_heads.astype(jnp.bfloat16)


def reference(queries, key_states, value_states, level_offsets, out_weight):
    def by_head(matrix):
        return matrix.reshape(TOKENS, HEADS, HD).transpose(1, 0, 2)

    mixed = lax.map(head_result, (by_head(queries), by_head(key_states), by_head(value_states), level_offsets.T))
    heads_out = mixed.transpose(1, 0, 2).reshape(TOKENS, HEADS * HD)
    return jnp.dot(heads_out, out_weight, preferred_element_type=jnp.float32).astype(jnp.bfloat16)
```

```python
import jax
import jax.numpy as jnp
from jax import lax
from jax.sharding import PartitionSpec as P

RATE_MID = 8
RATE_TOP = 32
SEG_ROWS = 1024
ROW = 16


NEG_FILL = -1e30


def send(array, pairs):
    return lax.ppermute(array, "seq", pairs)


def pick_rows(states, chooser, spacing):
    row_count, head_count, head_width = states.shape
    grouped = states.reshape(row_count // spacing, spacing, head_count, head_width)
    return jnp.einsum("nrhd,rh->nhd", grouped, chooser, preferred_element_type=jnp.float32).astype(
        jnp.bfloat16
    )


def attend(query_rows, key_rows, value_rows, allowed, scale_factor):
    scores = (
        jnp.einsum("qhd,khd->hqk", query_rows, key_rows, preferred_element_type=jnp.float32)
        * scale_factor
    )
    if allowed is not None:
        scores = jnp.where(allowed[None], scores, NEG_FILL)
    highest = jnp.max(scores, axis=2, keepdims=True)
    weights = jnp.exp(scores - highest)
    totals = jnp.sum(weights, axis=2, keepdims=True)
    shares = (weights / totals).astype(jnp.bfloat16)
    result = jnp.einsum("hqk,khd->qhd", shares, value_rows, preferred_element_type=jnp.float32)
    return (result, (highest + jnp.log(totals))[:, :, 0].T)


def merge(outs, lses):
    lse_stack = jnp.stack(lses)
    top = jnp.max(lse_stack, axis=0)
    weights = jnp.exp(lse_stack - top[None])
    total = jnp.sum(weights, axis=0)
    out = jnp.sum(weights[..., None] * jnp.stack(outs), axis=0) / total[..., None]
    return out, top + jnp.log(total)


def spread_back(level_out, level_lse, chooser):
    picked = chooser.astype(jnp.float32)
    sparse_count, head_count, head_width = level_out.shape
    row_count = sparse_count * chooser.shape[0]
    full_out = (level_out[:, None, :, :] * picked[None, :, :, None]).reshape(
        row_count, head_count, head_width
    )
    full_lse = jnp.where(chooser[None], level_lse[:, None, :], NEG_FILL).reshape(
        row_count, head_count
    )
    return (full_out, full_lse)


def level_setup(query_all, key_all, value_all, offset_row, spacing):
    head_count = query_all.shape[1]
    chooser = (
        lax.broadcasted_iota(jnp.int32, (spacing, head_count), 0) == (offset_row % spacing)[None, :]
    )
    chooser_bf = chooser.astype(jnp.bfloat16)
    query_rows = pick_rows(query_all, chooser_bf, spacing)
    pair_rows = jnp.stack(
        [pick_rows(key_all, chooser_bf, spacing), pick_rows(value_all, chooser_bf, spacing)], axis=1
    )
    return (chooser, query_rows, pair_rows)


def pack(out, lse):
    return jnp.concatenate([out, lse[..., None]], axis=-1)


def unpack(packed):
    return packed[..., :-1], packed[..., -1]


def ring_gather(block, seq_count):
    forward = [(s, (s // ROW) * ROW + (s % ROW + 1) % ROW) for s in range(seq_count)]
    backward = [(s, (s // ROW) * ROW + (s % ROW - 1) % ROW) for s in range(seq_count)]
    ahead = [None] * ROW
    ahead[0] = block
    moving = block
    for step in range(1, ROW // 2 + 1):
        moving = send(moving, forward)
        ahead[step] = moving
    moving = block
    for step in range(1, ROW // 2):
        moving = send(moving, backward)
        ahead[ROW - step] = moving
    return jnp.stack(ahead)


def local(queries, key_states, value_states, level_offsets, out_weight):
    row_count = queries.shape[0]
    head_count = level_offsets.shape[1]
    head_width = queries.shape[1] // head_count
    scale_factor = head_width ** (-0.5)
    seq_count = lax.axis_size("seq")
    seq_index = lax.axis_index("seq")
    row_y = seq_index // ROW
    row_z = seq_index % ROW
    rows_total = seq_count // ROW
    query_all = queries.reshape(row_count, head_count, head_width)
    key_all = key_states.reshape(row_count, head_count, head_width)
    value_all = value_states.reshape(row_count, head_count, head_width)
    full_outs = []
    full_lses = []

    span0 = SEG_ROWS // row_count
    chooser0, query0, pair0 = level_setup(query_all, key_all, value_all, level_offsets[0], 1)
    arrived = []
    for shift in range(span0 - 1, 0, -1):
        pairs = [(s, s + shift) for s in range(seq_count) if s % span0 + shift < span0]
        arrived.append(send(pair0, pairs))
    buffer0 = jnp.concatenate(arrived + [pair0], axis=0)
    shape0 = (row_count, span0 * row_count)
    key_index = lax.broadcasted_iota(jnp.int32, shape0, 1)
    query_index = lax.broadcasted_iota(jnp.int32, shape0, 0)
    lowest = (span0 - 1 - seq_index % span0) * row_count
    allowed0 = (key_index >= lowest) & (key_index <= (span0 - 1) * row_count + query_index)
    out0, lse0 = attend(query0, buffer0[:, 0], buffer0[:, 1], allowed0, scale_factor)
    full_out, full_lse = spread_back(out0, lse0, chooser0)
    full_outs.append(full_out)
    full_lses.append(full_lse)

    chooser1, query1, pair1 = level_setup(query_all, key_all, value_all, level_offsets[1], RATE_MID)
    chooser2, query2, pair2 = level_setup(query_all, key_all, value_all, level_offsets[2], RATE_TOP)
    count1 = pair1.shape[0]
    count2 = pair2.shape[0]
    ring = ring_gather(jnp.concatenate([pair1, pair2], axis=0), seq_count)
    row1 = ring[:, :count1]
    row2 = ring[:, count1:]

    def own_row(query_rows, row_blocks, count):
        keys = row_blocks.reshape(ROW * count, 2, head_count, head_width)
        shape = (count, ROW * count)
        key_index = lax.broadcasted_iota(jnp.int32, shape, 1)
        query_index = lax.broadcasted_iota(jnp.int32, shape, 0)
        offset = key_index // count
        allowed = jnp.where(
            offset == 0, key_index % count <= query_index, offset <= row_z
        )
        return attend(query_rows, keys[:, 0], keys[:, 1], allowed, scale_factor)

    def whole_row(query_rows, row_blocks, count):
        keys = row_blocks.reshape(ROW * count, 2, head_count, head_width)
        return attend(query_rows, keys[:, 0], keys[:, 1], None, scale_factor)

    up = [(s, s - ROW) for s in range(seq_count) if (s // ROW) % 2 == 1]
    down = [(s, s + ROW) for s in range(seq_count) if (s // ROW) % 2 == 0]
    visiting1 = send(query1, up)
    own_out1, own_lse1 = own_row(query1, row1, count1)
    cross1 = send(pack(*whole_row(visiting1, row1, count1)), down)
    cross_out1, cross_lse1 = unpack(cross1)
    cross_lse1 = jnp.where(row_y % 2 == 1, cross_lse1, NEG_FILL)
    out1, lse1 = merge([own_out1, cross_out1], [own_lse1, cross_lse1])
    full_out, full_lse = spread_back(out1, lse1, chooser1)
    full_outs.append(full_out)
    full_lses.append(full_lse)

    own_out2, own_lse2 = own_row(query2, row2, count2)
    visiting = []
    for gap in range(1, rows_total):
        pairs = [(s, s - gap * ROW) for s in range(seq_count) if s // ROW >= gap]
        visiting.append(send(query2, pairs))
    visiting2 = jnp.concatenate(visiting, axis=0)
    cross_out, cross_lse = whole_row(visiting2, row2, count2)
    outs2 = [own_out2]
    lses2 = [own_lse2]
    for gap in range(1, rows_total):
        pairs = [(s, s + gap * ROW) for s in range(seq_count) if s // ROW + gap < rows_total]
        part = slice((gap - 1) * count2, gap * count2)
        back_out, back_lse = unpack(send(pack(cross_out[part], cross_lse[part]), pairs))
        outs2.append(back_out)
        lses2.append(jnp.where(row_y >= gap, back_lse, NEG_FILL))
    out2, lse2 = merge(outs2, lses2)
    full_out, full_lse = spread_back(out2, lse2, chooser2)
    full_outs.append(full_out)
    full_lses.append(full_lse)

    lse_stack = jnp.stack(full_lses)
    level_top = jnp.max(lse_stack, axis=0)
    level_weights = jnp.exp(lse_stack - level_top[None])
    mixed_heads = (
        jnp.sum(level_weights[..., None] * jnp.stack(full_outs), axis=0)
        / jnp.sum(level_weights, axis=0)[..., None]
    )
    heads_out = mixed_heads.astype(jnp.bfloat16).reshape(row_count, head_count * head_width)
    projected = jnp.dot(
        lax.all_gather(heads_out, "head", axis=1, tiled=True),
        out_weight,
        preferred_element_type=jnp.float32,
    )
    return projected.astype(jnp.bfloat16)


def solution(mesh):
    return jax.shard_map(
        local,
        mesh=mesh,
        in_specs=(
            P("seq", "head"),
            P("seq", "head"),
            P("seq", "head"),
            P(None, "head"),
            P(None, "head"),
        ),
        out_specs=P("seq", "head"),
        check_vma=False,
    )
```

```python
import jax
import jax.numpy as jnp
from jax import lax
from jax.sharding import PartitionSpec as P

RATE_MID = 8
RATE_TOP = 32
SEG_ROWS = 1024
ROW = 16
TOK_DEV = 256


NEG_FILL = -1e30


def pick_rows(states, chooser, spacing):
    row_count, head_count, head_width = states.shape
    grouped = states.reshape(row_count // spacing, spacing, head_count, head_width)
    return jnp.einsum("nrhd,rh->nhd", grouped, chooser, preferred_element_type=jnp.float32).astype(
        jnp.bfloat16
    )


def attend(query_rows, key_rows, value_rows, allowed, scale_factor):
    scores = (
        jnp.einsum("qhd,khd->hqk", query_rows, key_rows, preferred_element_type=jnp.float32)
        * scale_factor
    )
    if allowed is not None:
        scores = jnp.where(allowed[None], scores, NEG_FILL)
    highest = jnp.max(scores, axis=2, keepdims=True)
    weights = jnp.exp(scores - highest)
    totals = jnp.sum(weights, axis=2, keepdims=True)
    shares = (weights / totals).astype(jnp.bfloat16)
    result = jnp.einsum("hqk,khd->qhd", shares, value_rows, preferred_element_type=jnp.float32)
    return (result, (highest + jnp.log(totals))[:, :, 0].T)


def merge(outs, lses):
    lse_stack = jnp.stack(lses)
    top = jnp.max(lse_stack, axis=0)
    weights = jnp.exp(lse_stack - top[None])
    total = jnp.sum(weights, axis=0)
    out = jnp.sum(weights[..., None] * jnp.stack(outs), axis=0) / total[..., None]
    return out, top + jnp.log(total)


def spread_back(level_out, level_lse, chooser):
    picked = chooser.astype(jnp.float32)
    sparse_count, head_count, head_width = level_out.shape
    row_count = sparse_count * chooser.shape[0]
    full_out = (level_out[:, None, :, :] * picked[None, :, :, None]).reshape(
        row_count, head_count, head_width
    )
    full_lse = jnp.where(chooser[None], level_lse[:, None, :], NEG_FILL).reshape(
        row_count, head_count
    )
    return (full_out, full_lse)


def level_setup(query_all, key_all, value_all, offset_row, spacing):
    head_count = query_all.shape[1]
    chooser = (
        lax.broadcasted_iota(jnp.int32, (spacing, head_count), 0) == (offset_row % spacing)[None, :]
    )
    chooser_bf = chooser.astype(jnp.bfloat16)
    query_rows = pick_rows(query_all, chooser_bf, spacing)
    pair_rows = jnp.stack(
        [pick_rows(key_all, chooser_bf, spacing), pick_rows(value_all, chooser_bf, spacing)], axis=1
    )
    return (chooser, query_rows, pair_rows)


def pack(out, lse):
    return jnp.concatenate([out, lse[..., None]], axis=-1)


def unpack(packed):
    return packed[..., :-1], packed[..., -1]


SEQ_AXES = ("sy", "sz")
ROW_AXES = "sz"


def split3(value):
    high = value.astype(jnp.bfloat16)
    rest = value - high.astype(jnp.float32)
    middle = rest.astype(jnp.bfloat16)
    low = (rest - middle.astype(jnp.float32)).astype(jnp.bfloat16)
    return jnp.stack([high, middle, low], axis=-1)


def join3(parts):
    parts = parts.astype(jnp.float32)
    return parts[..., 0] + parts[..., 1] + parts[..., 2]


def local(queries, key_states, value_states, level_offsets, out_weight):
    row_count = queries.shape[0]
    head_count = level_offsets.shape[1]
    head_width = queries.shape[1] // head_count
    scale_factor = head_width ** (-0.5)
    rows_total = lax.axis_size("sy")
    row_len = lax.axis_size("sz")
    seq_count = rows_total * row_len
    row_y = lax.axis_index("sy")
    row_z = lax.axis_index("sz")
    seq_index = row_y * row_len + row_z
    query_all = queries.reshape(row_count, head_count, head_width)
    key_all = key_states.reshape(row_count, head_count, head_width)
    value_all = value_states.reshape(row_count, head_count, head_width)
    full_outs = []
    full_lses = []

    span0 = SEG_ROWS // row_count
    chooser0, query0, pair0 = level_setup(query_all, key_all, value_all, level_offsets[0], 1)
    arrived = []
    for shift in range(span0 - 1, 0, -1):
        pairs = [(s, s + shift) for s in range(seq_count) if s % span0 + shift < span0]
        arrived.append(lax.ppermute(pair0, SEQ_AXES, pairs))
    buffer0 = jnp.concatenate(arrived + [pair0], axis=0)
    shape0 = (row_count, span0 * row_count)
    key_index = lax.broadcasted_iota(jnp.int32, shape0, 1)
    query_index = lax.broadcasted_iota(jnp.int32, shape0, 0)
    lowest = (span0 - 1 - seq_index % span0) * row_count
    allowed0 = (key_index >= lowest) & (key_index <= (span0 - 1) * row_count + query_index)
    out0, lse0 = attend(query0, buffer0[:, 0], buffer0[:, 1], allowed0, scale_factor)
    full_out, full_lse = spread_back(out0, lse0, chooser0)
    full_outs.append(full_out)
    full_lses.append(full_lse)

    chooser1, query1, pair1 = level_setup(query_all, key_all, value_all, level_offsets[1], RATE_MID)
    chooser2, query2, pair2 = level_setup(query_all, key_all, value_all, level_offsets[2], RATE_TOP)
    count1 = pair1.shape[0]
    count2 = pair2.shape[0]
    ring = lax.all_gather(jnp.concatenate([pair1, pair2], axis=0), ROW_AXES)
    row1 = ring[:, :count1]
    row2 = ring[:, count1:]

    def own_row(query_rows, row_blocks, count):
        keys = row_blocks.reshape(row_len * count, 2, head_count, head_width)
        shape = (count, row_len * count)
        key_index = lax.broadcasted_iota(jnp.int32, shape, 1)
        query_index = lax.broadcasted_iota(jnp.int32, shape, 0)
        source = key_index // count
        allowed = jnp.where(
            source == row_z, key_index % count <= query_index, source < row_z
        )
        return attend(query_rows, keys[:, 0], keys[:, 1], allowed, scale_factor)

    def whole_row(query_rows, row_blocks, count):
        keys = row_blocks.reshape(row_len * count, 2, head_count, head_width)
        return attend(query_rows, keys[:, 0], keys[:, 1], None, scale_factor)

    up = [(s, s - row_len) for s in range(seq_count) if (s // row_len) % 2 == 1]
    down = [(s, s + row_len) for s in range(seq_count) if (s // row_len) % 2 == 0]
    visiting1 = lax.ppermute(query1, SEQ_AXES, up)
    own_out1, own_lse1 = own_row(query1, row1, count1)
    cross1 = lax.ppermute(pack(*whole_row(visiting1, row1, count1)), SEQ_AXES, down)
    cross_out1, cross_lse1 = unpack(cross1)
    cross_lse1 = jnp.where(row_y % 2 == 1, cross_lse1, NEG_FILL)
    out1, lse1 = merge([own_out1, cross_out1], [own_lse1, cross_lse1])
    full_out, full_lse = spread_back(out1, lse1, chooser1)
    full_outs.append(full_out)
    full_lses.append(full_lse)

    own_out2, own_lse2 = own_row(query2, row2, count2)
    column_queries = lax.all_gather(query2, "sy", tiled=True)
    cross_out, cross_lse = whole_row(column_queries, row2, count2)
    packed = pack(cross_out, cross_lse).reshape(rows_total, count2, head_count, head_width + 1)
    returned = lax.all_to_all(packed, "sy", 0, 0, tiled=True)
    back_out, back_lse = unpack(returned)
    source_row = lax.broadcasted_iota(jnp.int32, back_lse.shape, 0)
    back_lse = jnp.where(source_row < row_y, back_lse, NEG_FILL)
    out2, lse2 = merge(
        [own_out2] + [back_out[i] for i in range(rows_total)],
        [own_lse2] + [back_lse[i] for i in range(rows_total)],
    )
    full_out, full_lse = spread_back(out2, lse2, chooser2)
    full_outs.append(full_out)
    full_lses.append(full_lse)

    lse_stack = jnp.stack(full_lses)
    level_top = jnp.max(lse_stack, axis=0)
    level_weights = jnp.exp(lse_stack - level_top[None])
    mixed_heads = (
        jnp.sum(level_weights[..., None] * jnp.stack(full_outs), axis=0)
        / jnp.sum(level_weights, axis=0)[..., None]
    )
    heads_out = mixed_heads.astype(jnp.bfloat16).reshape(row_count, head_count * head_width)
    projected = jnp.dot(
        lax.all_gather(heads_out, "head", axis=1, tiled=True),
        out_weight,
        preferred_element_type=jnp.float32,
    )
    return projected.astype(jnp.bfloat16)


def solution(mesh):
    seq_count, head_count = mesh.devices.shape
    split = jax.sharding.Mesh(
        mesh.devices.reshape(seq_count // ROW, ROW, head_count), SEQ_AXES + ("head",)
    )
    return jax.shard_map(
        local,
        mesh=split,
        in_specs=(
            P(SEQ_AXES, "head"),
            P(SEQ_AXES, "head"),
            P(SEQ_AXES, "head"),
            P(None, "head"),
            P(None, "head"),
        ),
        out_specs=P(SEQ_AXES, "head"),
        check_vma=False,
    )
```

```python
import jax
import jax.numpy as jnp
from jax import lax
from jax.sharding import PartitionSpec as P

RATE_MID = 8
RATE_TOP = 32
SEG_ROWS = 1024
ROW = 16
TOK_DEV = 256


NEG_FILL = -1e30


def pick_rows(states, chooser, spacing):
    row_count, head_count, head_width = states.shape
    grouped = states.reshape(row_count // spacing, spacing, head_count, head_width)
    return jnp.einsum("nrhd,rh->nhd", grouped, chooser, preferred_element_type=jnp.float32).astype(
        jnp.bfloat16
    )


def attend(query_rows, key_rows, value_rows, allowed, scale_factor):
    scores = (
        jnp.einsum("qhd,khd->hqk", query_rows, key_rows, preferred_element_type=jnp.float32)
        * scale_factor
    )
    if allowed is not None:
        scores = jnp.where(allowed[None], scores, NEG_FILL)
    highest = jnp.max(scores, axis=2, keepdims=True)
    weights = jnp.exp(scores - highest)
    totals = jnp.sum(weights, axis=2, keepdims=True)
    shares = (weights / totals).astype(jnp.bfloat16)
    result = jnp.einsum("hqk,khd->qhd", shares, value_rows, preferred_element_type=jnp.float32)
    return (result, (highest + jnp.log(totals))[:, :, 0].T)


def merge(outs, lses):
    lse_stack = jnp.stack(lses)
    top = jnp.max(lse_stack, axis=0)
    weights = jnp.exp(lse_stack - top[None])
    total = jnp.sum(weights, axis=0)
    out = jnp.sum(weights[..., None] * jnp.stack(outs), axis=0) / total[..., None]
    return out, top + jnp.log(total)


def spread_back(level_out, level_lse, chooser):
    picked = chooser.astype(jnp.float32)
    sparse_count, head_count, head_width = level_out.shape
    row_count = sparse_count * chooser.shape[0]
    full_out = (level_out[:, None, :, :] * picked[None, :, :, None]).reshape(
        row_count, head_count, head_width
    )
    full_lse = jnp.where(chooser[None], level_lse[:, None, :], NEG_FILL).reshape(
        row_count, head_count
    )
    return (full_out, full_lse)


def level_setup(query_all, key_all, value_all, offset_row, spacing):
    head_count = query_all.shape[1]
    chooser = (
        lax.broadcasted_iota(jnp.int32, (spacing, head_count), 0) == (offset_row % spacing)[None, :]
    )
    chooser_bf = chooser.astype(jnp.bfloat16)
    query_rows = pick_rows(query_all, chooser_bf, spacing)
    pair_rows = jnp.stack(
        [pick_rows(key_all, chooser_bf, spacing), pick_rows(value_all, chooser_bf, spacing)], axis=1
    )
    return (chooser, query_rows, pair_rows)


def pack(out, lse):
    return jnp.concatenate([out, lse[..., None]], axis=-1)


def unpack(packed):
    return packed[..., :-1], packed[..., -1]


SEQ_AXES = ("sy", "sz")
ROW_AXES = "sz"


def split3(value):
    high = value.astype(jnp.bfloat16)
    rest = value - high.astype(jnp.float32)
    middle = rest.astype(jnp.bfloat16)
    low = (rest - middle.astype(jnp.float32)).astype(jnp.bfloat16)
    return jnp.stack([high, middle, low], axis=-1)


def join3(parts):
    parts = parts.astype(jnp.float32)
    return parts[..., 0] + parts[..., 1] + parts[..., 2]


def local(queries, key_states, value_states, level_offsets, out_weight):
    row_count = queries.shape[0]
    head_count = level_offsets.shape[1]
    head_width = queries.shape[1] // head_count
    scale_factor = head_width ** (-0.5)
    rows_total = lax.axis_size("sy")
    row_len = lax.axis_size("sz")
    seq_count = rows_total * row_len
    row_y = lax.axis_index("sy")
    row_z = lax.axis_index("sz")
    seq_index = row_y * row_len + row_z
    query_all = queries.reshape(row_count, head_count, head_width)
    key_all = key_states.reshape(row_count, head_count, head_width)
    value_all = value_states.reshape(row_count, head_count, head_width)
    full_outs = []
    full_lses = []

    span0 = SEG_ROWS // row_count
    chooser0, query0, pair0 = level_setup(query_all, key_all, value_all, level_offsets[0], 1)
    arrived = []
    for shift in range(span0 - 1, 0, -1):
        pairs = [(s, s + shift) for s in range(seq_count) if s % span0 + shift < span0]
        arrived.append(lax.ppermute(pair0, SEQ_AXES, pairs))
    buffer0 = jnp.concatenate(arrived + [pair0], axis=0)
    shape0 = (row_count, span0 * row_count)
    key_index = lax.broadcasted_iota(jnp.int32, shape0, 1)
    query_index = lax.broadcasted_iota(jnp.int32, shape0, 0)
    lowest = (span0 - 1 - seq_index % span0) * row_count
    allowed0 = (key_index >= lowest) & (key_index <= (span0 - 1) * row_count + query_index)
    out0, lse0 = attend(query0, buffer0[:, 0], buffer0[:, 1], allowed0, scale_factor)
    full_out, full_lse = spread_back(out0, lse0, chooser0)
    full_outs.append(full_out)
    full_lses.append(full_lse)

    chooser1, query1, pair1 = level_setup(query_all, key_all, value_all, level_offsets[1], RATE_MID)
    chooser2, query2, pair2 = level_setup(query_all, key_all, value_all, level_offsets[2], RATE_TOP)
    count1 = pair1.shape[0]
    count2 = pair2.shape[0]
    ring = lax.all_gather(jnp.concatenate([pair1, pair2], axis=0), ROW_AXES)
    row1 = ring[:, :count1]
    row2 = ring[:, count1:]

    def own_row(query_rows, row_blocks, count):
        keys = row_blocks.reshape(row_len * count, 2, head_count, head_width)
        shape = (count, row_len * count)
        key_index = lax.broadcasted_iota(jnp.int32, shape, 1)
        query_index = lax.broadcasted_iota(jnp.int32, shape, 0)
        source = key_index // count
        allowed = jnp.where(
            source == row_z, key_index % count <= query_index, source < row_z
        )
        return attend(query_rows, keys[:, 0], keys[:, 1], allowed, scale_factor)

    def whole_row(query_rows, row_blocks, count):
        keys = row_blocks.reshape(row_len * count, 2, head_count, head_width)
        return attend(query_rows, keys[:, 0], keys[:, 1], None, scale_factor)

    up = [(s, s - row_len) for s in range(seq_count) if (s // row_len) % 2 == 1]
    down = [(s, s + row_len) for s in range(seq_count) if (s // row_len) % 2 == 0]
    visiting1 = lax.ppermute(query1, SEQ_AXES, up)
    own_out1, own_lse1 = own_row(query1, row1, count1)
    cross1 = lax.ppermute(pack(*whole_row(visiting1, row1, count1)), SEQ_AXES, down)
    cross_out1, cross_lse1 = unpack(cross1)
    cross_lse1 = jnp.where(row_y % 2 == 1, cross_lse1, NEG_FILL)
    out1, lse1 = merge([own_out1, cross_out1], [own_lse1, cross_lse1])
    full_out, full_lse = spread_back(out1, lse1, chooser1)
    full_outs.append(full_out)
    full_lses.append(full_lse)

    own_out2, own_lse2 = own_row(query2, row2, count2)
    visiting = [query2]
    for gap in range(1, rows_total):
        pairs = [(s, s - gap * row_len) for s in range(seq_count) if s // row_len >= gap]
        visiting.append(lax.ppermute(query2, SEQ_AXES, pairs))
    cross_out, cross_lse = whole_row(jnp.concatenate(visiting, axis=0), row2, count2)
    packed = pack(cross_out, cross_lse).reshape(rows_total, count2, head_count, head_width + 1)
    doubled = jnp.concatenate([packed, packed], axis=0)
    start = (rows_total - row_y) % rows_total
    packed = lax.dynamic_slice_in_dim(doubled, start, rows_total, axis=0)
    returned = lax.all_to_all(packed, "sy", 0, 0, tiled=True)
    back_out, back_lse = unpack(returned)
    source_row = lax.broadcasted_iota(jnp.int32, back_lse.shape, 0)
    back_lse = jnp.where(source_row < row_y, back_lse, NEG_FILL)
    out2, lse2 = merge(
        [own_out2] + [back_out[i] for i in range(rows_total)],
        [own_lse2] + [back_lse[i] for i in range(rows_total)],
    )
    full_out, full_lse = spread_back(out2, lse2, chooser2)
    full_outs.append(full_out)
    full_lses.append(full_lse)

    lse_stack = jnp.stack(full_lses)
    level_top = jnp.max(lse_stack, axis=0)
    level_weights = jnp.exp(lse_stack - level_top[None])
    mixed_heads = (
        jnp.sum(level_weights[..., None] * jnp.stack(full_outs), axis=0)
        / jnp.sum(level_weights, axis=0)[..., None]
    )
    heads_out = mixed_heads.astype(jnp.bfloat16).reshape(row_count, head_count * head_width)
    projected = jnp.dot(
        lax.all_gather(heads_out, "head", axis=1, tiled=True),
        out_weight,
        preferred_element_type=jnp.float32,
    )
    return projected.astype(jnp.bfloat16)


def solution(mesh):
    seq_count, head_count = mesh.devices.shape
    split = jax.sharding.Mesh(
        mesh.devices.reshape(seq_count // ROW, ROW, head_count), SEQ_AXES + ("head",)
    )
    return jax.shard_map(
        local,
        mesh=split,
        in_specs=(
            P(SEQ_AXES, "head"),
            P(SEQ_AXES, "head"),
            P(SEQ_AXES, "head"),
            P(None, "head"),
            P(None, "head"),
        ),
        out_specs=P(SEQ_AXES, "head"),
        check_vma=False,
    )
```

```python
import jax
import jax.numpy as jnp
from jax import lax
from jax.sharding import PartitionSpec as P

RATE_MID = 8
RATE_TOP = 32
SEG_ROWS = 1024
ROW = 16
TOK_DEV = 256


NEG_FILL = -1e30


def pick_rows(states, chooser, spacing):
    row_count, head_count, head_width = states.shape
    grouped = states.reshape(row_count // spacing, spacing, head_count, head_width)
    return jnp.einsum("nrhd,rh->nhd", grouped, chooser, preferred_element_type=jnp.float32).astype(
        jnp.bfloat16
    )


def attend(query_rows, key_rows, value_rows, allowed, scale_factor):
    scores = (
        jnp.einsum("qhd,khd->hqk", query_rows, key_rows, preferred_element_type=jnp.float32)
        * scale_factor
    )
    if allowed is not None:
        scores = jnp.where(allowed[None], scores, NEG_FILL)
    highest = jnp.max(scores, axis=2, keepdims=True)
    weights = jnp.exp(scores - highest)
    totals = jnp.sum(weights, axis=2, keepdims=True)
    shares = (weights / totals).astype(jnp.bfloat16)
    result = jnp.einsum("hqk,khd->qhd", shares, value_rows, preferred_element_type=jnp.float32)
    return (result, (highest + jnp.log(totals))[:, :, 0].T)


def merge(outs, lses):
    lse_stack = jnp.stack(lses)
    top = jnp.max(lse_stack, axis=0)
    weights = jnp.exp(lse_stack - top[None])
    total = jnp.sum(weights, axis=0)
    out = jnp.sum(weights[..., None] * jnp.stack(outs), axis=0) / total[..., None]
    return out, top + jnp.log(total)


def spread_back(level_out, level_lse, chooser):
    picked = chooser.astype(jnp.float32)
    sparse_count, head_count, head_width = level_out.shape
    row_count = sparse_count * chooser.shape[0]
    full_out = (level_out[:, None, :, :] * picked[None, :, :, None]).reshape(
        row_count, head_count, head_width
    )
    full_lse = jnp.where(chooser[None], level_lse[:, None, :], NEG_FILL).reshape(
        row_count, head_count
    )
    return (full_out, full_lse)


def level_setup(query_all, key_all, value_all, offset_row, spacing):
    head_count = query_all.shape[1]
    chooser = (
        lax.broadcasted_iota(jnp.int32, (spacing, head_count), 0) == (offset_row % spacing)[None, :]
    )
    chooser_bf = chooser.astype(jnp.bfloat16)
    query_rows = pick_rows(query_all, chooser_bf, spacing)
    pair_rows = jnp.stack(
        [pick_rows(key_all, chooser_bf, spacing), pick_rows(value_all, chooser_bf, spacing)], axis=1
    )
    return (chooser, query_rows, pair_rows)


def pack(out, lse):
    return jnp.concatenate([out, lse[..., None]], axis=-1)


def unpack(packed):
    return packed[..., :-1], packed[..., -1]


SEQ_AXES = ("sy", "sz")
ROW_AXES = "sz"


def split3(value):
    high = value.astype(jnp.bfloat16)
    rest = value - high.astype(jnp.float32)
    middle = rest.astype(jnp.bfloat16)
    low = (rest - middle.astype(jnp.float32)).astype(jnp.bfloat16)
    return jnp.stack([high, middle, low], axis=-1)


def join3(parts):
    parts = parts.astype(jnp.float32)
    return parts[..., 0] + parts[..., 1] + parts[..., 2]


def local(queries, key_states, value_states, level_offsets, out_weight):
    row_count = queries.shape[0]
    head_count = level_offsets.shape[1]
    head_width = queries.shape[1] // head_count
    scale_factor = head_width ** (-0.5)
    rows_total = lax.axis_size("sy")
    row_len = lax.axis_size("sz")
    seq_count = rows_total * row_len
    row_y = lax.axis_index("sy")
    row_z = lax.axis_index("sz")
    seq_index = row_y * row_len + row_z
    query_all = queries.reshape(row_count, head_count, head_width)
    key_all = key_states.reshape(row_count, head_count, head_width)
    value_all = value_states.reshape(row_count, head_count, head_width)
    full_outs = []
    full_lses = []

    span0 = SEG_ROWS // row_count
    chooser0, query0, pair0 = level_setup(query_all, key_all, value_all, level_offsets[0], 1)
    arrived = []
    for shift in range(span0 - 1, 0, -1):
        pairs = [(s, s + shift) for s in range(seq_count) if s % span0 + shift < span0]
        arrived.append(lax.ppermute(pair0, SEQ_AXES, pairs))
    buffer0 = jnp.concatenate(arrived + [pair0], axis=0)
    shape0 = (row_count, span0 * row_count)
    key_index = lax.broadcasted_iota(jnp.int32, shape0, 1)
    query_index = lax.broadcasted_iota(jnp.int32, shape0, 0)
    lowest = (span0 - 1 - seq_index % span0) * row_count
    allowed0 = (key_index >= lowest) & (key_index <= (span0 - 1) * row_count + query_index)
    out0, lse0 = attend(query0, buffer0[:, 0], buffer0[:, 1], allowed0, scale_factor)
    full_out, full_lse = spread_back(out0, lse0, chooser0)
    full_outs.append(full_out)
    full_lses.append(full_lse)

    chooser1, query1, pair1 = level_setup(query_all, key_all, value_all, level_offsets[1], RATE_MID)
    chooser2, query2, pair2 = level_setup(query_all, key_all, value_all, level_offsets[2], RATE_TOP)
    count1 = pair1.shape[0]
    count2 = pair2.shape[0]
    spare = jnp.zeros_like(pair2[:4])
    ring = lax.all_gather(jnp.concatenate([pair1, pair2, spare], axis=0), ROW_AXES)
    row1 = ring[:, :count1]
    row2 = ring[:, count1 : count1 + count2]

    def own_row(query_rows, row_blocks, count):
        keys = row_blocks.reshape(row_len * count, 2, head_count, head_width)
        shape = (count, row_len * count)
        key_index = lax.broadcasted_iota(jnp.int32, shape, 1)
        query_index = lax.broadcasted_iota(jnp.int32, shape, 0)
        source = key_index // count
        allowed = jnp.where(
            source == row_z, key_index % count <= query_index, source < row_z
        )
        return attend(query_rows, keys[:, 0], keys[:, 1], allowed, scale_factor)

    def whole_row(query_rows, row_blocks, count):
        keys = row_blocks.reshape(row_len * count, 2, head_count, head_width)
        return attend(query_rows, keys[:, 0], keys[:, 1], None, scale_factor)

    up = [(s, s - row_len) for s in range(seq_count) if (s // row_len) % 2 == 1]
    down = [(s, s + row_len) for s in range(seq_count) if (s // row_len) % 2 == 0]
    visiting1 = lax.ppermute(query1, SEQ_AXES, up)
    own_out1, own_lse1 = own_row(query1, row1, count1)
    cross1 = lax.ppermute(pack(*whole_row(visiting1, row1, count1)), SEQ_AXES, down)
    cross_out1, cross_lse1 = unpack(cross1)
    cross_lse1 = jnp.where(row_y % 2 == 1, cross_lse1, NEG_FILL)
    out1, lse1 = merge([own_out1, cross_out1], [own_lse1, cross_lse1])
    full_out, full_lse = spread_back(out1, lse1, chooser1)
    full_outs.append(full_out)
    full_lses.append(full_lse)

    own_out2, own_lse2 = own_row(query2, row2, count2)
    visiting = [query2]
    for gap in range(1, rows_total):
        pairs = [(s, s - gap * row_len) for s in range(seq_count) if s // row_len >= gap]
        visiting.append(lax.ppermute(query2, SEQ_AXES, pairs))
    cross_out, cross_lse = whole_row(jnp.concatenate(visiting, axis=0), row2, count2)
    packed = pack(cross_out, cross_lse).reshape(rows_total, count2, head_count, head_width + 1)
    doubled = jnp.concatenate([packed, packed], axis=0)
    start = (rows_total - row_y) % rows_total
    packed = lax.dynamic_slice_in_dim(doubled, start, rows_total, axis=0)
    returned = lax.all_to_all(packed, "sy", 0, 0, tiled=True)
    back_out, back_lse = unpack(returned)
    source_row = lax.broadcasted_iota(jnp.int32, back_lse.shape, 0)
    back_lse = jnp.where(source_row < row_y, back_lse, NEG_FILL)
    out2, lse2 = merge(
        [own_out2] + [back_out[i] for i in range(rows_total)],
        [own_lse2] + [back_lse[i] for i in range(rows_total)],
    )
    full_out, full_lse = spread_back(out2, lse2, chooser2)
    full_outs.append(full_out)
    full_lses.append(full_lse)

    lse_stack = jnp.stack(full_lses)
    level_top = jnp.max(lse_stack, axis=0)
    level_weights = jnp.exp(lse_stack - level_top[None])
    mixed_heads = (
        jnp.sum(level_weights[..., None] * jnp.stack(full_outs), axis=0)
        / jnp.sum(level_weights, axis=0)[..., None]
    )
    heads_out = mixed_heads.astype(jnp.bfloat16).reshape(row_count, head_count * head_width)
    projected = jnp.dot(
        lax.all_gather(heads_out, "head", axis=1, tiled=True),
        out_weight,
        preferred_element_type=jnp.float32,
    )
    return projected.astype(jnp.bfloat16)


def solution(mesh):
    seq_count, head_count = mesh.devices.shape
    split = jax.sharding.Mesh(
        mesh.devices.reshape(seq_count // ROW, ROW, head_count), SEQ_AXES + ("head",)
    )
    return jax.shard_map(
        local,
        mesh=split,
        in_specs=(
            P(SEQ_AXES, "head"),
            P(SEQ_AXES, "head"),
            P(SEQ_AXES, "head"),
            P(None, "head"),
            P(None, "head"),
        ),
        out_specs=P(SEQ_AXES, "head"),
        check_vma=False,
    )
```

```python
import jax
import jax.numpy as jnp
from jax import lax
from jax.sharding import PartitionSpec as P

RATE_MID = 8
RATE_TOP = 32
SEG_ROWS = 1024
ROW = 16
TOK_DEV = 256


NEG_FILL = -1e30


def pick_rows(states, chooser, spacing):
    row_count, head_count, head_width = states.shape
    grouped = states.reshape(row_count // spacing, spacing, head_count, head_width)
    return jnp.einsum("nrhd,rh->nhd", grouped, chooser, preferred_element_type=jnp.float32).astype(
        jnp.bfloat16
    )


def attend(query_rows, key_rows, value_rows, allowed, scale_factor):
    scores = (
        jnp.einsum("qhd,khd->hqk", query_rows, key_rows, preferred_element_type=jnp.float32)
        * scale_factor
    )
    if allowed is not None:
        scores = jnp.where(allowed[None], scores, NEG_FILL)
    highest = jnp.max(scores, axis=2, keepdims=True)
    weights = jnp.exp(scores - highest)
    totals = jnp.sum(weights, axis=2, keepdims=True)
    shares = (weights / totals).astype(jnp.bfloat16)
    result = jnp.einsum("hqk,khd->qhd", shares, value_rows, preferred_element_type=jnp.float32)
    return (result, (highest + jnp.log(totals))[:, :, 0].T)


def merge(outs, lses):
    lse_stack = jnp.stack(lses)
    top = jnp.max(lse_stack, axis=0)
    weights = jnp.exp(lse_stack - top[None])
    total = jnp.sum(weights, axis=0)
    out = jnp.sum(weights[..., None] * jnp.stack(outs), axis=0) / total[..., None]
    return out, top + jnp.log(total)


def spread_back(level_out, level_lse, chooser):
    picked = chooser.astype(jnp.float32)
    sparse_count, head_count, head_width = level_out.shape
    row_count = sparse_count * chooser.shape[0]
    full_out = (level_out[:, None, :, :] * picked[None, :, :, None]).reshape(
        row_count, head_count, head_width
    )
    full_lse = jnp.where(chooser[None], level_lse[:, None, :], NEG_FILL).reshape(
        row_count, head_count
    )
    return (full_out, full_lse)


def level_setup(query_all, key_all, value_all, offset_row, spacing):
    head_count = query_all.shape[1]
    chooser = (
        lax.broadcasted_iota(jnp.int32, (spacing, head_count), 0) == (offset_row % spacing)[None, :]
    )
    chooser_bf = chooser.astype(jnp.bfloat16)
    query_rows = pick_rows(query_all, chooser_bf, spacing)
    pair_rows = jnp.stack(
        [pick_rows(key_all, chooser_bf, spacing), pick_rows(value_all, chooser_bf, spacing)], axis=1
    )
    return (chooser, query_rows, pair_rows)


def pack(out, lse):
    return jnp.concatenate([out, lse[..., None]], axis=-1)


def unpack(packed):
    return packed[..., :-1], packed[..., -1]


SEQ_AXES = ("sy", "zh", "zl")


def split3(value):
    high = value.astype(jnp.bfloat16)
    rest = value - high.astype(jnp.float32)
    middle = rest.astype(jnp.bfloat16)
    low = (rest - middle.astype(jnp.float32)).astype(jnp.bfloat16)
    return jnp.stack([high, middle, low], axis=-1)


def join3(parts):
    parts = parts.astype(jnp.float32)
    return parts[..., 0] + parts[..., 1] + parts[..., 2]


def local(queries, key_states, value_states, level_offsets, out_weight):
    row_count = queries.shape[0]
    head_count = level_offsets.shape[1]
    head_width = queries.shape[1] // head_count
    scale_factor = head_width ** (-0.5)
    rows_total = lax.axis_size("sy")
    group = lax.axis_size("zl")
    row_len = group * lax.axis_size("zh")
    seq_count = rows_total * row_len
    row_y = lax.axis_index("sy")
    row_z = lax.axis_index("zh") * group + lax.axis_index("zl")
    seq_index = row_y * row_len + row_z
    query_all = queries.reshape(row_count, head_count, head_width)
    key_all = key_states.reshape(row_count, head_count, head_width)
    value_all = value_states.reshape(row_count, head_count, head_width)
    full_outs = []
    full_lses = []

    span0 = SEG_ROWS // row_count
    chooser0, query0, pair0 = level_setup(query_all, key_all, value_all, level_offsets[0], 1)
    arrived = []
    for shift in range(span0 - 1, 0, -1):
        pairs = [(s, s + shift) for s in range(seq_count) if s % span0 + shift < span0]
        arrived.append(lax.ppermute(pair0, SEQ_AXES, pairs))
    buffer0 = jnp.concatenate(arrived + [pair0], axis=0)
    shape0 = (row_count, span0 * row_count)
    key_index = lax.broadcasted_iota(jnp.int32, shape0, 1)
    query_index = lax.broadcasted_iota(jnp.int32, shape0, 0)
    lowest = (span0 - 1 - seq_index % span0) * row_count
    allowed0 = (key_index >= lowest) & (key_index <= (span0 - 1) * row_count + query_index)
    out0, lse0 = attend(query0, buffer0[:, 0], buffer0[:, 1], allowed0, scale_factor)
    full_out, full_lse = spread_back(out0, lse0, chooser0)
    full_outs.append(full_out)
    full_lses.append(full_lse)

    chooser1, query1, pair1 = level_setup(query_all, key_all, value_all, level_offsets[1], RATE_MID)
    chooser2, query2, pair2 = level_setup(query_all, key_all, value_all, level_offsets[2], RATE_TOP)
    count1 = pair1.shape[0]
    count2 = pair2.shape[0]
    ring = lax.all_gather(jnp.concatenate([pair1, pair2], axis=0), "zl")
    ring = lax.all_gather(ring, "zh").reshape(row_len, *ring.shape[1:])
    row1 = ring[:, :count1]
    row2 = ring[:, count1:]

    def own_row(query_rows, row_blocks, count):
        keys = row_blocks.reshape(row_len * count, 2, head_count, head_width)
        shape = (count, row_len * count)
        key_index = lax.broadcasted_iota(jnp.int32, shape, 1)
        query_index = lax.broadcasted_iota(jnp.int32, shape, 0)
        source = key_index // count
        allowed = jnp.where(
            source == row_z, key_index % count <= query_index, source < row_z
        )
        return attend(query_rows, keys[:, 0], keys[:, 1], allowed, scale_factor)

    def whole_row(query_rows, row_blocks, count):
        keys = row_blocks.reshape(row_len * count, 2, head_count, head_width)
        return attend(query_rows, keys[:, 0], keys[:, 1], None, scale_factor)

    up = [(s, s - row_len) for s in range(seq_count) if (s // row_len) % 2 == 1]
    down = [(s, s + row_len) for s in range(seq_count) if (s // row_len) % 2 == 0]
    visiting1 = lax.ppermute(query1, SEQ_AXES, up)
    own_out1, own_lse1 = own_row(query1, row1, count1)
    cross1 = lax.ppermute(pack(*whole_row(visiting1, row1, count1)), SEQ_AXES, down)
    cross_out1, cross_lse1 = unpack(cross1)
    cross_lse1 = jnp.where(row_y % 2 == 1, cross_lse1, NEG_FILL)
    out1, lse1 = merge([own_out1, cross_out1], [own_lse1, cross_lse1])
    full_out, full_lse = spread_back(out1, lse1, chooser1)
    full_outs.append(full_out)
    full_lses.append(full_lse)

    own_out2, own_lse2 = own_row(query2, row2, count2)
    copies = jnp.broadcast_to(query2[None], (rows_total,) + query2.shape)
    column_queries = lax.all_to_all(copies, "sy", 0, 0, tiled=True)
    cross_out, cross_lse = whole_row(
        column_queries.reshape(rows_total * count2, head_count, head_width), row2, count2
    )
    packed = pack(cross_out, cross_lse).reshape(rows_total, count2, head_count, head_width + 1)
    returned = lax.all_to_all(packed, "sy", 0, 0, tiled=True)
    back_out, back_lse = unpack(returned)
    source_row = lax.broadcasted_iota(jnp.int32, back_lse.shape, 0)
    back_lse = jnp.where(source_row < row_y, back_lse, NEG_FILL)
    out2, lse2 = merge(
        [own_out2] + [back_out[i] for i in range(rows_total)],
        [own_lse2] + [back_lse[i] for i in range(rows_total)],
    )
    full_out, full_lse = spread_back(out2, lse2, chooser2)
    full_outs.append(full_out)
    full_lses.append(full_lse)

    lse_stack = jnp.stack(full_lses)
    level_top = jnp.max(lse_stack, axis=0)
    level_weights = jnp.exp(lse_stack - level_top[None])
    mixed_heads = (
        jnp.sum(level_weights[..., None] * jnp.stack(full_outs), axis=0)
        / jnp.sum(level_weights, axis=0)[..., None]
    )
    heads_out = mixed_heads.astype(jnp.bfloat16).reshape(row_count, head_count * head_width)
    projected = jnp.dot(
        lax.all_gather(heads_out, "head", axis=1, tiled=True),
        out_weight,
        preferred_element_type=jnp.float32,
    )
    return projected.astype(jnp.bfloat16)


def solution(mesh):
    seq_count, head_count = mesh.devices.shape
    group = SEG_ROWS // TOK_DEV
    split = jax.sharding.Mesh(
        mesh.devices.reshape(seq_count // ROW, ROW // group, group, head_count),
        SEQ_AXES + ("head",),
    )
    return jax.shard_map(
        local,
        mesh=split,
        in_specs=(
            P(SEQ_AXES, "head"),
            P(SEQ_AXES, "head"),
            P(SEQ_AXES, "head"),
            P(None, "head"),
            P(None, "head"),
        ),
        out_specs=P(SEQ_AXES, "head"),
        check_vma=False,
    )
```

```python
import jax
import jax.numpy as jnp
from jax import lax
from jax.sharding import PartitionSpec as P

RATE_MID = 8
RATE_TOP = 32
SEG_ROWS = 1024
ROW = 16
TOK_DEV = 256


NEG_FILL = -1e30


def pick_rows(states, chooser, spacing):
    row_count, head_count, head_width = states.shape
    grouped = states.reshape(row_count // spacing, spacing, head_count, head_width)
    return jnp.einsum("nrhd,rh->nhd", grouped, chooser, preferred_element_type=jnp.float32).astype(
        jnp.bfloat16
    )


def attend(query_rows, key_rows, value_rows, allowed, scale_factor):
    scores = (
        jnp.einsum("qhd,khd->hqk", query_rows, key_rows, preferred_element_type=jnp.float32)
        * scale_factor
    )
    if allowed is not None:
        scores = jnp.where(allowed[None], scores, NEG_FILL)
    highest = jnp.max(scores, axis=2, keepdims=True)
    weights = jnp.exp(scores - highest)
    totals = jnp.sum(weights, axis=2, keepdims=True)
    shares = (weights / totals).astype(jnp.bfloat16)
    result = jnp.einsum("hqk,khd->qhd", shares, value_rows, preferred_element_type=jnp.float32)
    return (result, (highest + jnp.log(totals))[:, :, 0].T)


def merge(outs, lses):
    lse_stack = jnp.stack(lses)
    top = jnp.max(lse_stack, axis=0)
    weights = jnp.exp(lse_stack - top[None])
    total = jnp.sum(weights, axis=0)
    out = jnp.sum(weights[..., None] * jnp.stack(outs), axis=0) / total[..., None]
    return out, top + jnp.log(total)


def spread_back(level_out, level_lse, chooser):
    picked = chooser.astype(jnp.float32)
    sparse_count, head_count, head_width = level_out.shape
    row_count = sparse_count * chooser.shape[0]
    full_out = (level_out[:, None, :, :] * picked[None, :, :, None]).reshape(
        row_count, head_count, head_width
    )
    full_lse = jnp.where(chooser[None], level_lse[:, None, :], NEG_FILL).reshape(
        row_count, head_count
    )
    return (full_out, full_lse)


def level_setup(query_all, key_all, value_all, offset_row, spacing):
    head_count = query_all.shape[1]
    chooser = (
        lax.broadcasted_iota(jnp.int32, (spacing, head_count), 0) == (offset_row % spacing)[None, :]
    )
    chooser_bf = chooser.astype(jnp.bfloat16)
    query_rows = pick_rows(query_all, chooser_bf, spacing)
    pair_rows = jnp.stack(
        [pick_rows(key_all, chooser_bf, spacing), pick_rows(value_all, chooser_bf, spacing)], axis=1
    )
    return (chooser, query_rows, pair_rows)


def pack(out, lse):
    return jnp.concatenate([out, lse[..., None]], axis=-1)


def unpack(packed):
    return packed[..., :-1], packed[..., -1]


SEQ_AXES = ("sy", "zh", "zl")


def split3(value):
    high = value.astype(jnp.bfloat16)
    rest = value - high.astype(jnp.float32)
    middle = rest.astype(jnp.bfloat16)
    low = (rest - middle.astype(jnp.float32)).astype(jnp.bfloat16)
    return jnp.stack([high, middle, low], axis=-1)


def join3(parts):
    parts = parts.astype(jnp.float32)
    return parts[..., 0] + parts[..., 1] + parts[..., 2]


def local(queries, key_states, value_states, level_offsets, out_weight):
    row_count = queries.shape[0]
    head_count = level_offsets.shape[1]
    head_width = queries.shape[1] // head_count
    scale_factor = head_width ** (-0.5)
    rows_total = lax.axis_size("sy")
    group = lax.axis_size("zl")
    row_len = group * lax.axis_size("zh")
    seq_count = rows_total * row_len
    row_y = lax.axis_index("sy")
    row_z = lax.axis_index("zh") * group + lax.axis_index("zl")
    seq_index = row_y * row_len + row_z
    query_all = queries.reshape(row_count, head_count, head_width)
    key_all = key_states.reshape(row_count, head_count, head_width)
    value_all = value_states.reshape(row_count, head_count, head_width)
    full_outs = []
    full_lses = []

    span0 = SEG_ROWS // row_count
    chooser0, query0, pair0 = level_setup(query_all, key_all, value_all, level_offsets[0], 1)
    arrived = []
    for shift in range(span0 - 1, 0, -1):
        pairs = [(s, s + shift) for s in range(seq_count) if s % span0 + shift < span0]
        arrived.append(lax.ppermute(pair0, SEQ_AXES, pairs))
    buffer0 = jnp.concatenate(arrived + [pair0], axis=0)
    shape0 = (row_count, span0 * row_count)
    key_index = lax.broadcasted_iota(jnp.int32, shape0, 1)
    query_index = lax.broadcasted_iota(jnp.int32, shape0, 0)
    lowest = (span0 - 1 - seq_index % span0) * row_count
    allowed0 = (key_index >= lowest) & (key_index <= (span0 - 1) * row_count + query_index)
    out0, lse0 = attend(query0, buffer0[:, 0], buffer0[:, 1], allowed0, scale_factor)
    full_out, full_lse = spread_back(out0, lse0, chooser0)
    full_outs.append(full_out)
    full_lses.append(full_lse)

    chooser1, query1, pair1 = level_setup(query_all, key_all, value_all, level_offsets[1], RATE_MID)
    chooser2, query2, pair2 = level_setup(query_all, key_all, value_all, level_offsets[2], RATE_TOP)
    count1 = pair1.shape[0]
    count2 = pair2.shape[0]
    moving = jnp.concatenate([pair1, pair2], axis=0)
    backward = [
        (s, (s // row_len) * row_len + (s % row_len - 1) % row_len) for s in range(seq_count)
    ]
    held = [moving] + [None] * (row_len - 1)
    for step in range(1, row_len):
        moving = lax.ppermute(moving, SEQ_AXES, backward)
        held[row_len - step] = moving
    ring = jnp.stack(held)
    row1 = ring[:, :count1]
    row2 = ring[:, count1:]

    def own_row(query_rows, row_blocks, count):
        keys = row_blocks.reshape(row_len * count, 2, head_count, head_width)
        shape = (count, row_len * count)
        key_index = lax.broadcasted_iota(jnp.int32, shape, 1)
        query_index = lax.broadcasted_iota(jnp.int32, shape, 0)
        offset = key_index // count
        allowed = jnp.where(offset == 0, key_index % count <= query_index, offset <= row_z)
        return attend(query_rows, keys[:, 0], keys[:, 1], allowed, scale_factor)

    def whole_row(query_rows, row_blocks, count):
        keys = row_blocks.reshape(row_len * count, 2, head_count, head_width)
        return attend(query_rows, keys[:, 0], keys[:, 1], None, scale_factor)

    up = [(s, s - row_len) for s in range(seq_count) if (s // row_len) % 2 == 1]
    down = [(s, s + row_len) for s in range(seq_count) if (s // row_len) % 2 == 0]
    visiting1 = lax.ppermute(query1, SEQ_AXES, up)
    own_out1, own_lse1 = own_row(query1, row1, count1)
    cross1 = lax.ppermute(pack(*whole_row(visiting1, row1, count1)), SEQ_AXES, down)
    cross_out1, cross_lse1 = unpack(cross1)
    cross_lse1 = jnp.where(row_y % 2 == 1, cross_lse1, NEG_FILL)
    out1, lse1 = merge([own_out1, cross_out1], [own_lse1, cross_lse1])
    full_out, full_lse = spread_back(out1, lse1, chooser1)
    full_outs.append(full_out)
    full_lses.append(full_lse)

    own_out2, own_lse2 = own_row(query2, row2, count2)
    copies = jnp.broadcast_to(query2[None], (rows_total,) + query2.shape)
    column_queries = lax.all_to_all(copies, "sy", 0, 0, tiled=True)
    cross_out, cross_lse = whole_row(
        column_queries.reshape(rows_total * count2, head_count, head_width), row2, count2
    )
    packed = pack(cross_out, cross_lse).reshape(rows_total, count2, head_count, head_width + 1)
    returned = lax.all_to_all(packed, "sy", 0, 0, tiled=True)
    back_out, back_lse = unpack(returned)
    source_row = lax.broadcasted_iota(jnp.int32, back_lse.shape, 0)
    back_lse = jnp.where(source_row < row_y, back_lse, NEG_FILL)
    out2, lse2 = merge(
        [own_out2] + [back_out[i] for i in range(rows_total)],
        [own_lse2] + [back_lse[i] for i in range(rows_total)],
    )
    full_out, full_lse = spread_back(out2, lse2, chooser2)
    full_outs.append(full_out)
    full_lses.append(full_lse)

    lse_stack = jnp.stack(full_lses)
    level_top = jnp.max(lse_stack, axis=0)
    level_weights = jnp.exp(lse_stack - level_top[None])
    mixed_heads = (
        jnp.sum(level_weights[..., None] * jnp.stack(full_outs), axis=0)
        / jnp.sum(level_weights, axis=0)[..., None]
    )
    heads_out = mixed_heads.astype(jnp.bfloat16).reshape(row_count, head_count * head_width)
    projected = jnp.dot(
        lax.all_gather(heads_out, "head", axis=1, tiled=True),
        out_weight,
        preferred_element_type=jnp.float32,
    )
    return projected.astype(jnp.bfloat16)


def solution(mesh):
    seq_count, head_count = mesh.devices.shape
    group = SEG_ROWS // TOK_DEV
    split = jax.sharding.Mesh(
        mesh.devices.reshape(seq_count // ROW, ROW // group, group, head_count),
        SEQ_AXES + ("head",),
    )
    return jax.shard_map(
        local,
        mesh=split,
        in_specs=(
            P(SEQ_AXES, "head"),
            P(SEQ_AXES, "head"),
            P(SEQ_AXES, "head"),
            P(None, "head"),
            P(None, "head"),
        ),
        out_specs=P(SEQ_AXES, "head"),
        check_vma=False,
    )
```

```python
import jax
import jax.numpy as jnp
from jax import lax
from jax.sharding import PartitionSpec as P

RATE_MID = 8
RATE_TOP = 32
SEG_ROWS = 1024
ROW = 16
TOK_DEV = 256


NEG_FILL = -1e30


def pick_rows(states, chooser, spacing):
    row_count, head_count, head_width = states.shape
    grouped = states.reshape(row_count // spacing, spacing, head_count, head_width)
    return jnp.einsum("nrhd,rh->nhd", grouped, chooser, preferred_element_type=jnp.float32).astype(
        jnp.bfloat16
    )


def attend(query_rows, key_rows, value_rows, allowed, scale_factor):
    scores = (
        jnp.einsum("qhd,khd->hqk", query_rows, key_rows, preferred_element_type=jnp.float32)
        * scale_factor
    )
    if allowed is not None:
        scores = jnp.where(allowed[None], scores, NEG_FILL)
    highest = jnp.max(scores, axis=2, keepdims=True)
    weights = jnp.exp(scores - highest)
    totals = jnp.sum(weights, axis=2, keepdims=True)
    shares = (weights / totals).astype(jnp.bfloat16)
    result = jnp.einsum("hqk,khd->qhd", shares, value_rows, preferred_element_type=jnp.float32)
    return (result, (highest + jnp.log(totals))[:, :, 0].T)


def merge(outs, lses):
    lse_stack = jnp.stack(lses)
    top = jnp.max(lse_stack, axis=0)
    weights = jnp.exp(lse_stack - top[None])
    total = jnp.sum(weights, axis=0)
    out = jnp.sum(weights[..., None] * jnp.stack(outs), axis=0) / total[..., None]
    return out, top + jnp.log(total)


def spread_back(level_out, level_lse, chooser):
    picked = chooser.astype(jnp.float32)
    sparse_count, head_count, head_width = level_out.shape
    row_count = sparse_count * chooser.shape[0]
    full_out = (level_out[:, None, :, :] * picked[None, :, :, None]).reshape(
        row_count, head_count, head_width
    )
    full_lse = jnp.where(chooser[None], level_lse[:, None, :], NEG_FILL).reshape(
        row_count, head_count
    )
    return (full_out, full_lse)


def level_setup(query_all, key_all, value_all, offset_row, spacing):
    head_count = query_all.shape[1]
    chooser = (
        lax.broadcasted_iota(jnp.int32, (spacing, head_count), 0) == (offset_row % spacing)[None, :]
    )
    chooser_bf = chooser.astype(jnp.bfloat16)
    query_rows = pick_rows(query_all, chooser_bf, spacing)
    pair_rows = jnp.stack(
        [pick_rows(key_all, chooser_bf, spacing), pick_rows(value_all, chooser_bf, spacing)], axis=1
    )
    return (chooser, query_rows, pair_rows)


def pack(out, lse):
    return jnp.concatenate([out, lse[..., None]], axis=-1)


def unpack(packed):
    return packed[..., :-1], packed[..., -1]


SEQ_AXES = ("sy", "zh", "zl")


def split3(value):
    high = value.astype(jnp.bfloat16)
    rest = value - high.astype(jnp.float32)
    middle = rest.astype(jnp.bfloat16)
    low = (rest - middle.astype(jnp.float32)).astype(jnp.bfloat16)
    return jnp.stack([high, middle, low], axis=-1)


def join3(parts):
    parts = parts.astype(jnp.float32)
    return parts[..., 0] + parts[..., 1] + parts[..., 2]


def local(queries, key_states, value_states, level_offsets, out_weight):
    row_count = queries.shape[0]
    head_count = level_offsets.shape[1]
    head_width = queries.shape[1] // head_count
    scale_factor = head_width ** (-0.5)
    rows_total = lax.axis_size("sy")
    group = lax.axis_size("zl")
    row_len = group * lax.axis_size("zh")
    seq_count = rows_total * row_len
    row_y = lax.axis_index("sy")
    row_z = lax.axis_index("zh") * group + lax.axis_index("zl")
    seq_index = row_y * row_len + row_z
    query_all = queries.reshape(row_count, head_count, head_width)
    key_all = key_states.reshape(row_count, head_count, head_width)
    value_all = value_states.reshape(row_count, head_count, head_width)
    full_outs = []
    full_lses = []

    span0 = SEG_ROWS // row_count
    chooser0, query0, pair0 = level_setup(query_all, key_all, value_all, level_offsets[0], 1)
    arrived = []
    for shift in range(span0 - 1, 0, -1):
        pairs = [(s, s + shift) for s in range(seq_count) if s % span0 + shift < span0]
        arrived.append(lax.ppermute(pair0, SEQ_AXES, pairs))
    buffer0 = jnp.concatenate(arrived + [pair0], axis=0)
    shape0 = (row_count, span0 * row_count)
    key_index = lax.broadcasted_iota(jnp.int32, shape0, 1)
    query_index = lax.broadcasted_iota(jnp.int32, shape0, 0)
    lowest = (span0 - 1 - seq_index % span0) * row_count
    allowed0 = (key_index >= lowest) & (key_index <= (span0 - 1) * row_count + query_index)
    out0, lse0 = attend(query0, buffer0[:, 0], buffer0[:, 1], allowed0, scale_factor)
    full_out, full_lse = spread_back(out0, lse0, chooser0)
    full_outs.append(full_out)
    full_lses.append(full_lse)

    chooser1, query1, pair1 = level_setup(query_all, key_all, value_all, level_offsets[1], RATE_MID)
    chooser2, query2, pair2 = level_setup(query_all, key_all, value_all, level_offsets[2], RATE_TOP)
    count1 = pair1.shape[0]
    count2 = pair2.shape[0]
    ring = lax.all_gather(jnp.concatenate([pair1, pair2], axis=0), ("zh", "zl"))
    row1 = ring[:, :count1]
    row2 = ring[:, count1:]

    def own_row(query_rows, row_blocks, count):
        keys = row_blocks.reshape(row_len * count, 2, head_count, head_width)
        shape = (count, row_len * count)
        key_index = lax.broadcasted_iota(jnp.int32, shape, 1)
        query_index = lax.broadcasted_iota(jnp.int32, shape, 0)
        source = key_index // count
        allowed = jnp.where(
            source == row_z, key_index % count <= query_index, source < row_z
        )
        return attend(query_rows, keys[:, 0], keys[:, 1], allowed, scale_factor)

    def whole_row(query_rows, row_blocks, count):
        keys = row_blocks.reshape(row_len * count, 2, head_count, head_width)
        return attend(query_rows, keys[:, 0], keys[:, 1], None, scale_factor)

    up = [(s, s - row_len) for s in range(seq_count) if (s // row_len) % 2 == 1]
    down = [(s, s + row_len) for s in range(seq_count) if (s // row_len) % 2 == 0]
    visiting1 = lax.ppermute(query1, SEQ_AXES, up)
    own_out1, own_lse1 = own_row(query1, row1, count1)
    cross1 = lax.ppermute(pack(*whole_row(visiting1, row1, count1)), SEQ_AXES, down)
    cross_out1, cross_lse1 = unpack(cross1)
    cross_lse1 = jnp.where(row_y % 2 == 1, cross_lse1, NEG_FILL)
    out1, lse1 = merge([own_out1, cross_out1], [own_lse1, cross_lse1])
    full_out, full_lse = spread_back(out1, lse1, chooser1)
    full_outs.append(full_out)
    full_lses.append(full_lse)

    own_out2, own_lse2 = own_row(query2, row2, count2)
    copies = jnp.broadcast_to(query2[None], (rows_total,) + query2.shape)
    column_queries = lax.all_to_all(copies, "sy", 0, 0, tiled=True)
    cross_out, cross_lse = whole_row(
        column_queries.reshape(rows_total * count2, head_count, head_width), row2, count2
    )
    packed = pack(cross_out, cross_lse).reshape(rows_total, count2, head_count, head_width + 1)
    returned = lax.all_to_all(packed, "sy", 0, 0, tiled=True)
    back_out, back_lse = unpack(returned)
    source_row = lax.broadcasted_iota(jnp.int32, back_lse.shape, 0)
    back_lse = jnp.where(source_row < row_y, back_lse, NEG_FILL)
    out2, lse2 = merge(
        [own_out2] + [back_out[i] for i in range(rows_total)],
        [own_lse2] + [back_lse[i] for i in range(rows_total)],
    )
    full_out, full_lse = spread_back(out2, lse2, chooser2)
    full_outs.append(full_out)
    full_lses.append(full_lse)

    lse_stack = jnp.stack(full_lses)
    level_top = jnp.max(lse_stack, axis=0)
    level_weights = jnp.exp(lse_stack - level_top[None])
    mixed_heads = (
        jnp.sum(level_weights[..., None] * jnp.stack(full_outs), axis=0)
        / jnp.sum(level_weights, axis=0)[..., None]
    )
    heads_out = mixed_heads.astype(jnp.bfloat16).reshape(row_count, head_count * head_width)
    projected = jnp.dot(
        lax.all_gather(heads_out, "head", axis=1, tiled=True),
        out_weight,
        preferred_element_type=jnp.float32,
    )
    return projected.astype(jnp.bfloat16)


def solution(mesh):
    seq_count, head_count = mesh.devices.shape
    group = SEG_ROWS // TOK_DEV
    split = jax.sharding.Mesh(
        mesh.devices.reshape(seq_count // ROW, ROW // group, group, head_count),
        SEQ_AXES + ("head",),
    )
    return jax.shard_map(
        local,
        mesh=split,
        in_specs=(
            P(SEQ_AXES, "head"),
            P(SEQ_AXES, "head"),
            P(SEQ_AXES, "head"),
            P(None, "head"),
            P(None, "head"),
        ),
        out_specs=P(SEQ_AXES, "head"),
        check_vma=False,
    )
```

```python
import jax
import jax.numpy as jnp
from jax import lax
from jax.sharding import PartitionSpec as P

RATE_MID = 8
RATE_TOP = 32
SEG_ROWS = 1024
ROW = 16
TOK_DEV = 256


NEG_FILL = -1e30


def pick_rows(states, chooser, spacing):
    row_count, head_count, head_width = states.shape
    grouped = states.reshape(row_count // spacing, spacing, head_count, head_width)
    return jnp.einsum("nrhd,rh->nhd", grouped, chooser, preferred_element_type=jnp.float32).astype(
        jnp.bfloat16
    )


def attend(query_rows, key_rows, value_rows, allowed, scale_factor):
    scores = (
        jnp.einsum("qhd,khd->hqk", query_rows, key_rows, preferred_element_type=jnp.float32)
        * scale_factor
    )
    if allowed is not None:
        scores = jnp.where(allowed[None], scores, NEG_FILL)
    highest = jnp.max(scores, axis=2, keepdims=True)
    weights = jnp.exp(scores - highest)
    totals = jnp.sum(weights, axis=2, keepdims=True)
    shares = (weights / totals).astype(jnp.bfloat16)
    result = jnp.einsum("hqk,khd->qhd", shares, value_rows, preferred_element_type=jnp.float32)
    return (result, (highest + jnp.log(totals))[:, :, 0].T)


def merge(outs, lses):
    lse_stack = jnp.stack(lses)
    top = jnp.max(lse_stack, axis=0)
    weights = jnp.exp(lse_stack - top[None])
    total = jnp.sum(weights, axis=0)
    out = jnp.sum(weights[..., None] * jnp.stack(outs), axis=0) / total[..., None]
    return out, top + jnp.log(total)


def spread_back(level_out, level_lse, chooser):
    picked = chooser.astype(jnp.float32)
    sparse_count, head_count, head_width = level_out.shape
    row_count = sparse_count * chooser.shape[0]
    full_out = (level_out[:, None, :, :] * picked[None, :, :, None]).reshape(
        row_count, head_count, head_width
    )
    full_lse = jnp.where(chooser[None], level_lse[:, None, :], NEG_FILL).reshape(
        row_count, head_count
    )
    return (full_out, full_lse)


def level_setup(query_all, key_all, value_all, offset_row, spacing):
    head_count = query_all.shape[1]
    chooser = (
        lax.broadcasted_iota(jnp.int32, (spacing, head_count), 0) == (offset_row % spacing)[None, :]
    )
    chooser_bf = chooser.astype(jnp.bfloat16)
    query_rows = pick_rows(query_all, chooser_bf, spacing)
    pair_rows = jnp.stack(
        [pick_rows(key_all, chooser_bf, spacing), pick_rows(value_all, chooser_bf, spacing)], axis=1
    )
    return (chooser, query_rows, pair_rows)


def pack(out, lse):
    return jnp.concatenate([out, lse[..., None]], axis=-1)


def unpack(packed):
    return packed[..., :-1], packed[..., -1]


SEQ_AXES = ("sy", "zh", "zl")


def split3(value):
    high = value.astype(jnp.bfloat16)
    rest = value - high.astype(jnp.float32)
    middle = rest.astype(jnp.bfloat16)
    low = (rest - middle.astype(jnp.float32)).astype(jnp.bfloat16)
    return jnp.stack([high, middle, low], axis=-1)


def join3(parts):
    parts = parts.astype(jnp.float32)
    return parts[..., 0] + parts[..., 1] + parts[..., 2]


def local(queries, key_states, value_states, level_offsets, out_weight):
    row_count = queries.shape[0]
    head_count = level_offsets.shape[1]
    head_width = queries.shape[1] // head_count
    scale_factor = head_width ** (-0.5)
    rows_total = lax.axis_size("sy")
    group = lax.axis_size("zl")
    row_len = group * lax.axis_size("zh")
    seq_count = rows_total * row_len
    row_y = lax.axis_index("sy")
    row_z = lax.axis_index("zh") * group + lax.axis_index("zl")
    seq_index = row_y * row_len + row_z
    query_all = queries.reshape(row_count, head_count, head_width)
    key_all = key_states.reshape(row_count, head_count, head_width)
    value_all = value_states.reshape(row_count, head_count, head_width)
    full_outs = []
    full_lses = []

    span0 = SEG_ROWS // row_count
    chooser0, query0, pair0 = level_setup(query_all, key_all, value_all, level_offsets[0], 1)
    arrived = []
    for shift in range(span0 - 1, 0, -1):
        pairs = [(s, s + shift) for s in range(seq_count) if s % span0 + shift < span0]
        arrived.append(lax.ppermute(pair0, SEQ_AXES, pairs))
    buffer0 = jnp.concatenate(arrived + [pair0], axis=0)
    shape0 = (row_count, span0 * row_count)
    key_index = lax.broadcasted_iota(jnp.int32, shape0, 1)
    query_index = lax.broadcasted_iota(jnp.int32, shape0, 0)
    lowest = (span0 - 1 - seq_index % span0) * row_count
    allowed0 = (key_index >= lowest) & (key_index <= (span0 - 1) * row_count + query_index)
    out0, lse0 = attend(query0, buffer0[:, 0], buffer0[:, 1], allowed0, scale_factor)
    full_out, full_lse = spread_back(out0, lse0, chooser0)
    full_outs.append(full_out)
    full_lses.append(full_lse)

    chooser1, query1, pair1 = level_setup(query_all, key_all, value_all, level_offsets[1], RATE_MID)
    chooser2, query2, pair2 = level_setup(query_all, key_all, value_all, level_offsets[2], RATE_TOP)
    count1 = pair1.shape[0]
    count2 = pair2.shape[0]
    ring = lax.all_gather(jnp.concatenate([pair1, pair2], axis=0), ("zh", "zl"))
    row1 = ring[:, :count1]
    row2 = ring[:, count1:]

    def own_row(query_rows, row_blocks, count):
        keys = row_blocks.reshape(row_len * count, 2, head_count, head_width)
        shape = (count, row_len * count)
        key_index = lax.broadcasted_iota(jnp.int32, shape, 1)
        query_index = lax.broadcasted_iota(jnp.int32, shape, 0)
        source = key_index // count
        allowed = jnp.where(
            source == row_z, key_index % count <= query_index, source < row_z
        )
        return attend(query_rows, keys[:, 0], keys[:, 1], allowed, scale_factor)

    def whole_row(query_rows, row_blocks, count):
        keys = row_blocks.reshape(row_len * count, 2, head_count, head_width)
        return attend(query_rows, keys[:, 0], keys[:, 1], None, scale_factor)

    up = [(s, s - row_len) for s in range(seq_count) if (s // row_len) % 2 == 1]
    down = [(s, s + row_len) for s in range(seq_count) if (s // row_len) % 2 == 0]
    visiting1 = lax.ppermute(query1, SEQ_AXES, up)
    own_out1, own_lse1 = own_row(query1, row1, count1)
    early = full_outs[0].astype(jnp.bfloat16)
    early, cross_send = lax.optimization_barrier(
        (early, pack(*whole_row(visiting1, row1, count1)))
    )
    cross1 = lax.ppermute(cross_send, SEQ_AXES, down)
    cross_out1, cross_lse1 = unpack(cross1)
    cross_lse1 = jnp.where(row_y % 2 == 1, cross_lse1, NEG_FILL)
    out1, lse1 = merge([own_out1, cross_out1], [own_lse1, cross_lse1])
    full_out, full_lse = spread_back(out1, lse1, chooser1)
    full_outs.append(full_out)
    full_lses.append(full_lse)

    own_out2, own_lse2 = own_row(query2, row2, count2)
    copies = jnp.broadcast_to(query2[None], (rows_total,) + query2.shape)
    column_queries = lax.all_to_all(copies, "sy", 0, 0, tiled=True)
    cross_out, cross_lse = whole_row(
        column_queries.reshape(rows_total * count2, head_count, head_width), row2, count2
    )
    packed = pack(cross_out, cross_lse).reshape(rows_total, count2, head_count, head_width + 1)
    returned = lax.all_to_all(packed, "sy", 0, 0, tiled=True)
    back_out, back_lse = unpack(returned)
    source_row = lax.broadcasted_iota(jnp.int32, back_lse.shape, 0)
    back_lse = jnp.where(source_row < row_y, back_lse, NEG_FILL)
    out2, lse2 = merge(
        [own_out2] + [back_out[i] for i in range(rows_total)],
        [own_lse2] + [back_lse[i] for i in range(rows_total)],
    )
    full_out, full_lse = spread_back(out2, lse2, chooser2)
    full_outs.append(full_out)
    full_lses.append(full_lse)

    lse_stack = jnp.stack(full_lses)
    level_top = jnp.max(lse_stack, axis=0)
    level_weights = jnp.exp(lse_stack - level_top[None])
    mixed_heads = (
        jnp.sum(level_weights[..., None] * jnp.stack(full_outs), axis=0)
        / jnp.sum(level_weights, axis=0)[..., None]
    )
    heads_out = mixed_heads.astype(jnp.bfloat16)

    early_all = lax.all_gather(
        early.reshape(row_count, head_count * head_width), "head", axis=1, tiled=True
    )
    projected = jnp.dot(early_all, out_weight, preferred_element_type=jnp.float32)
    delta = heads_out.astype(jnp.float32) - early.astype(jnp.float32)

    def take(dense, chooser, spacing):
        grouped = dense.reshape(row_count // spacing, spacing, head_count, head_width)
        return jnp.sum(jnp.where(chooser[None, :, :, None], grouped, 0.0), axis=1)

    is_mid = jnp.tile(chooser1, (row_count // RATE_MID, 1))
    picked = jnp.concatenate(
        [
            take(delta, chooser1, RATE_MID),
            take(jnp.where(is_mid[..., None], 0.0, delta), chooser2, RATE_TOP),
        ],
        axis=0,
    )
    picked_all = lax.all_gather(picked, "head", axis=1, tiled=True)
    offsets_all = lax.all_gather(level_offsets, "head", axis=1, tiled=True)
    heads_total = offsets_all.shape[1]
    weight = out_weight.reshape(heads_total, head_width, out_weight.shape[1])
    exact = lax.Precision.HIGHEST
    products = jnp.einsum(
        "nhd,hdc->hnc", picked_all, weight.astype(jnp.float32), precision=exact
    )
    mid_hot = (
        lax.broadcasted_iota(jnp.int32, (heads_total, RATE_MID), 1)
        == (offsets_all[1] % RATE_MID)[:, None]
    ).astype(jnp.float32)
    top_hot = (
        lax.broadcasted_iota(jnp.int32, (heads_total, RATE_TOP), 1)
        == (offsets_all[2] % RATE_TOP)[:, None]
    ).astype(jnp.float32)
    fix_mid = jnp.einsum("hnc,hr->nrc", products[:, :count1], mid_hot, precision=exact)
    fix_top = jnp.einsum("hnc,hr->nrc", products[:, count1:], top_hot, precision=exact)
    projected = (
        projected
        + fix_mid.reshape(row_count, -1)
        + fix_top.reshape(row_count, -1)
    )
    return projected.astype(jnp.bfloat16)


def solution(mesh):
    seq_count, head_count = mesh.devices.shape
    group = SEG_ROWS // TOK_DEV
    split = jax.sharding.Mesh(
        mesh.devices.reshape(seq_count // ROW, ROW // group, group, head_count),
        SEQ_AXES + ("head",),
    )
    return jax.shard_map(
        local,
        mesh=split,
        in_specs=(
            P(SEQ_AXES, "head"),
            P(SEQ_AXES, "head"),
            P(SEQ_AXES, "head"),
            P(None, "head"),
            P(None, "head"),
        ),
        out_specs=P(SEQ_AXES, "head"),
        check_vma=False,
    )
```

```python
import jax
import jax.numpy as jnp
from jax import lax
from jax.sharding import PartitionSpec as P

RATE_MID = 8
RATE_TOP = 32
SEG_ROWS = 1024
ROW = 16
TOK_DEV = 256


NEG_FILL = -1e30


def pick_rows(states, chooser, spacing):
    row_count, head_count, head_width = states.shape
    grouped = states.reshape(row_count // spacing, spacing, head_count, head_width)
    return jnp.einsum("nrhd,rh->nhd", grouped, chooser, preferred_element_type=jnp.float32).astype(
        jnp.bfloat16
    )


def attend(query_rows, key_rows, value_rows, allowed, scale_factor):
    scores = (
        jnp.einsum("qhd,khd->hqk", query_rows, key_rows, preferred_element_type=jnp.float32)
        * scale_factor
    )
    if allowed is not None:
        scores = jnp.where(allowed[None], scores, NEG_FILL)
    highest = jnp.max(scores, axis=2, keepdims=True)
    weights = jnp.exp(scores - highest)
    totals = jnp.sum(weights, axis=2, keepdims=True)
    shares = (weights / totals).astype(jnp.bfloat16)
    result = jnp.einsum("hqk,khd->qhd", shares, value_rows, preferred_element_type=jnp.float32)
    return (result, (highest + jnp.log(totals))[:, :, 0].T)


def merge(outs, lses):
    lse_stack = jnp.stack(lses)
    top = jnp.max(lse_stack, axis=0)
    weights = jnp.exp(lse_stack - top[None])
    total = jnp.sum(weights, axis=0)
    out = jnp.sum(weights[..., None] * jnp.stack(outs), axis=0) / total[..., None]
    return out, top + jnp.log(total)


def spread_back(level_out, level_lse, chooser):
    picked = chooser.astype(jnp.float32)
    sparse_count, head_count, head_width = level_out.shape
    row_count = sparse_count * chooser.shape[0]
    full_out = (level_out[:, None, :, :] * picked[None, :, :, None]).reshape(
        row_count, head_count, head_width
    )
    full_lse = jnp.where(chooser[None], level_lse[:, None, :], NEG_FILL).reshape(
        row_count, head_count
    )
    return (full_out, full_lse)


def level_setup(query_all, key_all, value_all, offset_row, spacing):
    head_count = query_all.shape[1]
    chooser = (
        lax.broadcasted_iota(jnp.int32, (spacing, head_count), 0) == (offset_row % spacing)[None, :]
    )
    chooser_bf = chooser.astype(jnp.bfloat16)
    query_rows = pick_rows(query_all, chooser_bf, spacing)
    pair_rows = jnp.stack(
        [pick_rows(key_all, chooser_bf, spacing), pick_rows(value_all, chooser_bf, spacing)], axis=1
    )
    return (chooser, query_rows, pair_rows)


def pack(out, lse):
    return jnp.concatenate([out, lse[..., None]], axis=-1)


def unpack(packed):
    return packed[..., :-1], packed[..., -1]


SEQ_AXES = ("sy", "sz")
ROW_AXES = "sz"


def split3(value):
    high = value.astype(jnp.bfloat16)
    rest = value - high.astype(jnp.float32)
    middle = rest.astype(jnp.bfloat16)
    low = (rest - middle.astype(jnp.float32)).astype(jnp.bfloat16)
    return jnp.stack([high, middle, low], axis=-1)


def join3(parts):
    parts = parts.astype(jnp.float32)
    return parts[..., 0] + parts[..., 1] + parts[..., 2]


def local(queries, key_states, value_states, level_offsets, out_weight):
    row_count = queries.shape[0]
    head_count = level_offsets.shape[1]
    head_width = queries.shape[1] // head_count
    scale_factor = head_width ** (-0.5)
    rows_total = lax.axis_size("sy")
    row_len = lax.axis_size("sz")
    seq_count = rows_total * row_len
    row_y = lax.axis_index("sy")
    row_z = lax.axis_index("sz")
    seq_index = row_y * row_len + row_z
    query_all = queries.reshape(row_count, head_count, head_width)
    key_all = key_states.reshape(row_count, head_count, head_width)
    value_all = value_states.reshape(row_count, head_count, head_width)
    full_outs = []
    full_lses = []

    span0 = SEG_ROWS // row_count
    chooser0, query0, pair0 = level_setup(query_all, key_all, value_all, level_offsets[0], 1)
    arrived = []
    for shift in range(span0 - 1, 0, -1):
        pairs = [(s, s + shift) for s in range(seq_count) if s % span0 + shift < span0]
        arrived.append(lax.ppermute(pair0, SEQ_AXES, pairs))
    buffer0 = jnp.concatenate(arrived + [pair0], axis=0)
    shape0 = (row_count, span0 * row_count)
    key_index = lax.broadcasted_iota(jnp.int32, shape0, 1)
    query_index = lax.broadcasted_iota(jnp.int32, shape0, 0)
    lowest = (span0 - 1 - seq_index % span0) * row_count
    allowed0 = (key_index >= lowest) & (key_index <= (span0 - 1) * row_count + query_index)
    out0, lse0 = attend(query0, buffer0[:, 0], buffer0[:, 1], allowed0, scale_factor)
    full_out, full_lse = spread_back(out0, lse0, chooser0)
    full_outs.append(full_out)
    full_lses.append(full_lse)

    chooser1, query1, pair1 = level_setup(query_all, key_all, value_all, level_offsets[1], RATE_MID)
    chooser2, query2, pair2 = level_setup(query_all, key_all, value_all, level_offsets[2], RATE_TOP)
    count1 = pair1.shape[0]
    count2 = pair2.shape[0]
    ring = lax.all_gather(jnp.concatenate([pair1, pair2], axis=0), ROW_AXES)
    row1 = ring[:, :count1]
    row2 = ring[:, count1:]

    def own_row(query_rows, row_blocks, count):
        keys = row_blocks.reshape(row_len * count, 2, head_count, head_width)
        shape = (count, row_len * count)
        key_index = lax.broadcasted_iota(jnp.int32, shape, 1)
        query_index = lax.broadcasted_iota(jnp.int32, shape, 0)
        source = key_index // count
        allowed = jnp.where(
            source == row_z, key_index % count <= query_index, source < row_z
        )
        return attend(query_rows, keys[:, 0], keys[:, 1], allowed, scale_factor)

    def whole_row(query_rows, row_blocks, count):
        keys = row_blocks.reshape(row_len * count, 2, head_count, head_width)
        return attend(query_rows, keys[:, 0], keys[:, 1], None, scale_factor)

    up = [(s, s - row_len) for s in range(seq_count) if (s // row_len) % 2 == 1]
    down = [(s, s + row_len) for s in range(seq_count) if (s // row_len) % 2 == 0]
    visiting1 = lax.ppermute(query1, SEQ_AXES, up)
    own_out1, own_lse1 = own_row(query1, row1, count1)
    cross1 = lax.ppermute(pack(*whole_row(visiting1, row1, count1)), SEQ_AXES, down)
    cross_out1, cross_lse1 = unpack(cross1)
    cross_lse1 = jnp.where(row_y % 2 == 1, cross_lse1, NEG_FILL)
    out1, lse1 = merge([own_out1, cross_out1], [own_lse1, cross_lse1])
    full_out, full_lse = spread_back(out1, lse1, chooser1)
    full_outs.append(full_out)
    full_lses.append(full_lse)

    own_out2, own_lse2 = own_row(query2, row2, count2)
    visiting = [query2]
    for gap in range(1, rows_total):
        pairs = [(s, s - gap * row_len) for s in range(seq_count) if s // row_len >= gap]
        visiting.append(lax.ppermute(query2, SEQ_AXES, pairs))
    cross_out, cross_lse = whole_row(jnp.concatenate(visiting, axis=0), row2, count2)
    packed = pack(cross_out, cross_lse).reshape(rows_total, count2, head_count, head_width + 1)
    doubled = jnp.concatenate([packed, packed], axis=0)
    start = (rows_total - row_y) % rows_total
    packed = lax.dynamic_slice_in_dim(doubled, start, rows_total, axis=0)
    returned = lax.all_to_all(packed, "sy", 0, 0, tiled=True)
    back_out, back_lse = unpack(returned)
    source_row = lax.broadcasted_iota(jnp.int32, back_lse.shape, 0)
    back_lse = jnp.where(source_row < row_y, back_lse, NEG_FILL)
    out2, lse2 = merge(
        [own_out2] + [back_out[i] for i in range(rows_total)],
        [own_lse2] + [back_lse[i] for i in range(rows_total)],
    )
    full_out, full_lse = spread_back(out2, lse2, chooser2)
    full_outs.append(full_out)
    full_lses.append(full_lse)

    lse_stack = jnp.stack(full_lses)
    level_top = jnp.max(lse_stack, axis=0)
    level_weights = jnp.exp(lse_stack - level_top[None])
    mixed_heads = (
        jnp.sum(level_weights[..., None] * jnp.stack(full_outs), axis=0)
        / jnp.sum(level_weights, axis=0)[..., None]
    )
    heads_out = mixed_heads.astype(jnp.bfloat16).reshape(row_count, head_count * head_width)
    head_devices = lax.axis_size("head")
    copies = jnp.broadcast_to(heads_out[None], (head_devices,) + heads_out.shape)
    gathered = lax.all_to_all(copies, "head", 0, 0, tiled=True)
    weight = out_weight.reshape(head_devices, head_count * head_width, out_weight.shape[1])
    projected = jnp.einsum(
        "str,sro->to", gathered, weight, preferred_element_type=jnp.float32
    )
    return projected.astype(jnp.bfloat16)


def solution(mesh):
    seq_count, head_count = mesh.devices.shape
    split = jax.sharding.Mesh(
        mesh.devices.reshape(seq_count // ROW, ROW, head_count), SEQ_AXES + ("head",)
    )
    return jax.shard_map(
        local,
        mesh=split,
        in_specs=(
            P(SEQ_AXES, "head"),
            P(SEQ_AXES, "head"),
            P(SEQ_AXES, "head"),
            P(None, "head"),
            P(None, "head"),
        ),
        out_specs=P(SEQ_AXES, "head"),
        check_vma=False,
    )
```

```python
import jax
import jax.numpy as jnp
from jax import lax
from jax.sharding import PartitionSpec as P

RATE_MID = 8
RATE_TOP = 32
SEG_ROWS = 1024
ROW = 16
TOK_DEV = 256


NEG_FILL = -1e30


def pick_rows(states, chooser, spacing):
    row_count, head_count, head_width = states.shape
    grouped = states.reshape(row_count // spacing, spacing, head_count, head_width)
    return jnp.einsum("nrhd,rh->nhd", grouped, chooser, preferred_element_type=jnp.float32).astype(
        jnp.bfloat16
    )


def attend(query_rows, key_rows, value_rows, allowed, scale_factor):
    scores = (
        jnp.einsum("qhd,khd->hqk", query_rows, key_rows, preferred_element_type=jnp.float32)
        * scale_factor
    )
    if allowed is not None:
        scores = jnp.where(allowed[None], scores, NEG_FILL)
    highest = jnp.max(scores, axis=2, keepdims=True)
    weights = jnp.exp(scores - highest)
    totals = jnp.sum(weights, axis=2, keepdims=True)
    shares = (weights / totals).astype(jnp.bfloat16)
    result = jnp.einsum("hqk,khd->qhd", shares, value_rows, preferred_element_type=jnp.float32)
    return (result, (highest + jnp.log(totals))[:, :, 0].T)


def merge(outs, lses):
    lse_stack = jnp.stack(lses)
    top = jnp.max(lse_stack, axis=0)
    weights = jnp.exp(lse_stack - top[None])
    total = jnp.sum(weights, axis=0)
    out = jnp.sum(weights[..., None] * jnp.stack(outs), axis=0) / total[..., None]
    return out, top + jnp.log(total)


def spread_back(level_out, level_lse, chooser):
    picked = chooser.astype(jnp.float32)
    sparse_count, head_count, head_width = level_out.shape
    row_count = sparse_count * chooser.shape[0]
    full_out = (level_out[:, None, :, :] * picked[None, :, :, None]).reshape(
        row_count, head_count, head_width
    )
    full_lse = jnp.where(chooser[None], level_lse[:, None, :], NEG_FILL).reshape(
        row_count, head_count
    )
    return (full_out, full_lse)


def level_setup(query_all, key_all, value_all, offset_row, spacing):
    head_count = query_all.shape[1]
    chooser = (
        lax.broadcasted_iota(jnp.int32, (spacing, head_count), 0) == (offset_row % spacing)[None, :]
    )
    chooser_bf = chooser.astype(jnp.bfloat16)
    query_rows = pick_rows(query_all, chooser_bf, spacing)
    pair_rows = jnp.stack(
        [pick_rows(key_all, chooser_bf, spacing), pick_rows(value_all, chooser_bf, spacing)], axis=1
    )
    return (chooser, query_rows, pair_rows)


def pack(out, lse):
    return jnp.concatenate([out, lse[..., None]], axis=-1)


def unpack(packed):
    return packed[..., :-1], packed[..., -1]


SEQ_AXES = ("sy", "sz")
ROW_AXES = "sz"


def split3(value):
    high = value.astype(jnp.bfloat16)
    rest = value - high.astype(jnp.float32)
    middle = rest.astype(jnp.bfloat16)
    low = (rest - middle.astype(jnp.float32)).astype(jnp.bfloat16)
    return jnp.stack([high, middle, low], axis=-1)


def join3(parts):
    parts = parts.astype(jnp.float32)
    return parts[..., 0] + parts[..., 1] + parts[..., 2]


def local(queries, key_states, value_states, level_offsets, out_weight):
    row_count = queries.shape[0]
    head_count = level_offsets.shape[1]
    head_width = queries.shape[1] // head_count
    scale_factor = head_width ** (-0.5)
    rows_total = lax.axis_size("sy")
    row_len = lax.axis_size("sz")
    seq_count = rows_total * row_len
    row_y = lax.axis_index("sy")
    row_z = lax.axis_index("sz")
    seq_index = row_y * row_len + row_z
    query_all = queries.reshape(row_count, head_count, head_width)
    key_all = key_states.reshape(row_count, head_count, head_width)
    value_all = value_states.reshape(row_count, head_count, head_width)
    full_outs = []
    full_lses = []

    chooser1, query1, pair1 = level_setup(query_all, key_all, value_all, level_offsets[1], RATE_MID)
    chooser2, query2, pair2 = level_setup(query_all, key_all, value_all, level_offsets[2], RATE_TOP)
    count1 = pair1.shape[0]
    count2 = pair2.shape[0]
    ring = lax.all_gather(jnp.concatenate([pair1, pair2], axis=0), ROW_AXES)
    row1 = ring[:, :count1]

    span0 = SEG_ROWS // row_count
    chooser0, query0, pair0 = level_setup(query_all, key_all, value_all, level_offsets[0], 1)
    pair0, ring = lax.optimization_barrier((pair0, ring))
    arrived = []
    for shift in range(span0 - 1, 0, -1):
        pairs = [(s, s + shift) for s in range(seq_count) if s % span0 + shift < span0]
        arrived.append(lax.ppermute(pair0, SEQ_AXES, pairs))
    buffer0 = jnp.concatenate(arrived + [pair0], axis=0)
    shape0 = (row_count, span0 * row_count)
    key_index = lax.broadcasted_iota(jnp.int32, shape0, 1)
    query_index = lax.broadcasted_iota(jnp.int32, shape0, 0)
    lowest = (span0 - 1 - seq_index % span0) * row_count
    allowed0 = (key_index >= lowest) & (key_index <= (span0 - 1) * row_count + query_index)
    out0, lse0 = attend(query0, buffer0[:, 0], buffer0[:, 1], allowed0, scale_factor)
    full_out, full_lse = spread_back(out0, lse0, chooser0)
    full_outs.append(full_out)
    full_lses.append(full_lse)

    row2 = ring[:, count1:]

    def own_row(query_rows, row_blocks, count):
        keys = row_blocks.reshape(row_len * count, 2, head_count, head_width)
        shape = (count, row_len * count)
        key_index = lax.broadcasted_iota(jnp.int32, shape, 1)
        query_index = lax.broadcasted_iota(jnp.int32, shape, 0)
        source = key_index // count
        allowed = jnp.where(
            source == row_z, key_index % count <= query_index, source < row_z
        )
        return attend(query_rows, keys[:, 0], keys[:, 1], allowed, scale_factor)

    def whole_row(query_rows, row_blocks, count):
        keys = row_blocks.reshape(row_len * count, 2, head_count, head_width)
        return attend(query_rows, keys[:, 0], keys[:, 1], None, scale_factor)

    up = [(s, s - row_len) for s in range(seq_count) if (s // row_len) % 2 == 1]
    down = [(s, s + row_len) for s in range(seq_count) if (s // row_len) % 2 == 0]
    visiting1 = lax.ppermute(query1, SEQ_AXES, up)
    own_out1, own_lse1 = own_row(query1, row1, count1)
    cross1 = lax.ppermute(pack(*whole_row(visiting1, row1, count1)), SEQ_AXES, down)
    cross_out1, cross_lse1 = unpack(cross1)
    cross_lse1 = jnp.where(row_y % 2 == 1, cross_lse1, NEG_FILL)
    out1, lse1 = merge([own_out1, cross_out1], [own_lse1, cross_lse1])
    full_out, full_lse = spread_back(out1, lse1, chooser1)
    full_outs.append(full_out)
    full_lses.append(full_lse)

    own_out2, own_lse2 = own_row(query2, row2, count2)
    copies = jnp.broadcast_to(query2[None], (rows_total,) + query2.shape)
    column_queries = lax.all_to_all(copies, "sy", 0, 0, tiled=True)
    cross_out, cross_lse = whole_row(
        column_queries.reshape(rows_total * count2, head_count, head_width), row2, count2
    )
    packed = pack(cross_out, cross_lse).reshape(rows_total, count2, head_count, head_width + 1)
    returned = lax.all_to_all(packed, "sy", 0, 0, tiled=True)
    back_out, back_lse = unpack(returned)
    source_row = lax.broadcasted_iota(jnp.int32, back_lse.shape, 0)
    back_lse = jnp.where(source_row < row_y, back_lse, NEG_FILL)
    out2, lse2 = merge(
        [own_out2] + [back_out[i] for i in range(rows_total)],
        [own_lse2] + [back_lse[i] for i in range(rows_total)],
    )
    full_out, full_lse = spread_back(out2, lse2, chooser2)
    full_outs.append(full_out)
    full_lses.append(full_lse)

    lse_stack = jnp.stack(full_lses)
    level_top = jnp.max(lse_stack, axis=0)
    level_weights = jnp.exp(lse_stack - level_top[None])
    mixed_heads = (
        jnp.sum(level_weights[..., None] * jnp.stack(full_outs), axis=0)
        / jnp.sum(level_weights, axis=0)[..., None]
    )
    heads_out = mixed_heads.astype(jnp.bfloat16).reshape(row_count, head_count * head_width)
    head_devices = lax.axis_size("head")
    copies = jnp.broadcast_to(heads_out[None], (head_devices,) + heads_out.shape)
    gathered = lax.all_to_all(copies, "head", 0, 0, tiled=True)
    weight = out_weight.reshape(head_devices, head_count * head_width, out_weight.shape[1])
    projected = jnp.einsum(
        "str,sro->to", gathered, weight, preferred_element_type=jnp.float32
    )
    return projected.astype(jnp.bfloat16)


def solution(mesh):
    seq_count, head_count = mesh.devices.shape
    split = jax.sharding.Mesh(
        mesh.devices.reshape(seq_count // ROW, ROW, head_count), SEQ_AXES + ("head",)
    )
    return jax.shard_map(
        local,
        mesh=split,
        in_specs=(
            P(SEQ_AXES, "head"),
            P(SEQ_AXES, "head"),
            P(SEQ_AXES, "head"),
            P(None, "head"),
            P(None, "head"),
        ),
        out_specs=P(SEQ_AXES, "head"),
        check_vma=False,
    )
```

```python
import jax
import jax.numpy as jnp
from jax import lax
from jax.sharding import PartitionSpec as P

RATE_MID = 8
RATE_TOP = 32
SEG_ROWS = 1024
ROW = 16
TOK_DEV = 256


NEG_FILL = -1e30


def pick_rows(states, chooser, spacing):
    row_count, head_count, head_width = states.shape
    grouped = states.reshape(row_count // spacing, spacing, head_count, head_width)
    return jnp.einsum("nrhd,rh->nhd", grouped, chooser, preferred_element_type=jnp.float32).astype(
        jnp.bfloat16
    )


def attend(query_rows, key_rows, value_rows, allowed, scale_factor):
    scores = (
        jnp.einsum("qhd,khd->hqk", query_rows, key_rows, preferred_element_type=jnp.float32)
        * scale_factor
    )
    if allowed is not None:
        scores = jnp.where(allowed[None], scores, NEG_FILL)
    highest = jnp.max(scores, axis=2, keepdims=True)
    weights = jnp.exp(scores - highest)
    totals = jnp.sum(weights, axis=2, keepdims=True)
    shares = (weights / totals).astype(jnp.bfloat16)
    result = jnp.einsum("hqk,khd->qhd", shares, value_rows, preferred_element_type=jnp.float32)
    return (result, (highest + jnp.log(totals))[:, :, 0].T)


def merge(outs, lses):
    lse_stack = jnp.stack(lses)
    top = jnp.max(lse_stack, axis=0)
    weights = jnp.exp(lse_stack - top[None])
    total = jnp.sum(weights, axis=0)
    out = jnp.sum(weights[..., None] * jnp.stack(outs), axis=0) / total[..., None]
    return out, top + jnp.log(total)


def spread_back(level_out, level_lse, chooser):
    picked = chooser.astype(jnp.float32)
    sparse_count, head_count, head_width = level_out.shape
    row_count = sparse_count * chooser.shape[0]
    full_out = (level_out[:, None, :, :] * picked[None, :, :, None]).reshape(
        row_count, head_count, head_width
    )
    full_lse = jnp.where(chooser[None], level_lse[:, None, :], NEG_FILL).reshape(
        row_count, head_count
    )
    return (full_out, full_lse)


def level_setup(query_all, key_all, value_all, offset_row, spacing):
    head_count = query_all.shape[1]
    chooser = (
        lax.broadcasted_iota(jnp.int32, (spacing, head_count), 0) == (offset_row % spacing)[None, :]
    )
    chooser_bf = chooser.astype(jnp.bfloat16)
    query_rows = pick_rows(query_all, chooser_bf, spacing)
    pair_rows = jnp.stack(
        [pick_rows(key_all, chooser_bf, spacing), pick_rows(value_all, chooser_bf, spacing)], axis=1
    )
    return (chooser, query_rows, pair_rows)


def pack(out, lse):
    return jnp.concatenate([out, lse[..., None]], axis=-1)


def unpack(packed):
    return packed[..., :-1], packed[..., -1]


SEQ_AXES = ("sy", "sz")
HEAD_AXES = ("hx", "hc")
ROW_AXES = "sz"


def split3(value):
    high = value.astype(jnp.bfloat16)
    rest = value - high.astype(jnp.float32)
    middle = rest.astype(jnp.bfloat16)
    low = (rest - middle.astype(jnp.float32)).astype(jnp.bfloat16)
    return jnp.stack([high, middle, low], axis=-1)


def join3(parts):
    parts = parts.astype(jnp.float32)
    return parts[..., 0] + parts[..., 1] + parts[..., 2]


def local(queries, key_states, value_states, level_offsets, out_weight):
    row_count = queries.shape[0]
    head_count = level_offsets.shape[1]
    head_width = queries.shape[1] // head_count
    scale_factor = head_width ** (-0.5)
    rows_total = lax.axis_size("sy")
    row_len = lax.axis_size("sz")
    seq_count = rows_total * row_len
    row_y = lax.axis_index("sy")
    row_z = lax.axis_index("sz")
    seq_index = row_y * row_len + row_z
    query_all = queries.reshape(row_count, head_count, head_width)
    key_all = key_states.reshape(row_count, head_count, head_width)
    value_all = value_states.reshape(row_count, head_count, head_width)
    full_outs = []
    full_lses = []

    span0 = SEG_ROWS // row_count
    chooser0, query0, pair0 = level_setup(query_all, key_all, value_all, level_offsets[0], 1)
    arrived = []
    for shift in range(span0 - 1, 0, -1):
        pairs = [(s, s + shift) for s in range(seq_count) if s % span0 + shift < span0]
        arrived.append(lax.ppermute(pair0, SEQ_AXES, pairs))
    buffer0 = jnp.concatenate(arrived + [pair0], axis=0)
    shape0 = (row_count, span0 * row_count)
    key_index = lax.broadcasted_iota(jnp.int32, shape0, 1)
    query_index = lax.broadcasted_iota(jnp.int32, shape0, 0)
    lowest = (span0 - 1 - seq_index % span0) * row_count
    allowed0 = (key_index >= lowest) & (key_index <= (span0 - 1) * row_count + query_index)
    out0, lse0 = attend(query0, buffer0[:, 0], buffer0[:, 1], allowed0, scale_factor)
    full_out, full_lse = spread_back(out0, lse0, chooser0)
    full_outs.append(full_out)
    full_lses.append(full_lse)

    chooser1, query1, pair1 = level_setup(query_all, key_all, value_all, level_offsets[1], RATE_MID)
    chooser2, query2, pair2 = level_setup(query_all, key_all, value_all, level_offsets[2], RATE_TOP)
    count1 = pair1.shape[0]
    count2 = pair2.shape[0]
    ring = lax.all_gather(jnp.concatenate([pair1, pair2], axis=0), ROW_AXES)
    row1 = ring[:, :count1]
    row2 = ring[:, count1:]

    def own_row(query_rows, row_blocks, count):
        keys = row_blocks.reshape(row_len * count, 2, head_count, head_width)
        shape = (count, row_len * count)
        key_index = lax.broadcasted_iota(jnp.int32, shape, 1)
        query_index = lax.broadcasted_iota(jnp.int32, shape, 0)
        source = key_index // count
        allowed = jnp.where(
            source == row_z, key_index % count <= query_index, source < row_z
        )
        return attend(query_rows, keys[:, 0], keys[:, 1], allowed, scale_factor)

    def whole_row(query_rows, row_blocks, count):
        keys = row_blocks.reshape(row_len * count, 2, head_count, head_width)
        return attend(query_rows, keys[:, 0], keys[:, 1], None, scale_factor)

    up = [(s, s - row_len) for s in range(seq_count) if (s // row_len) % 2 == 1]
    down = [(s, s + row_len) for s in range(seq_count) if (s // row_len) % 2 == 0]
    visiting1 = lax.ppermute(query1, SEQ_AXES, up)
    own_out1, own_lse1 = own_row(query1, row1, count1)
    cross1 = lax.ppermute(pack(*whole_row(visiting1, row1, count1)), SEQ_AXES, down)
    cross_out1, cross_lse1 = unpack(cross1)
    cross_lse1 = jnp.where(row_y % 2 == 1, cross_lse1, NEG_FILL)
    out1, lse1 = merge([own_out1, cross_out1], [own_lse1, cross_lse1])
    full_out, full_lse = spread_back(out1, lse1, chooser1)
    full_outs.append(full_out)
    full_lses.append(full_lse)

    own_out2, own_lse2 = own_row(query2, row2, count2)
    visiting = [query2]
    for gap in range(1, rows_total):
        pairs = [(s, s - gap * row_len) for s in range(seq_count) if s // row_len >= gap]
        visiting.append(lax.ppermute(query2, SEQ_AXES, pairs))
    cross_out, cross_lse = whole_row(jnp.concatenate(visiting, axis=0), row2, count2)
    packed = pack(cross_out, cross_lse).reshape(rows_total, count2, head_count, head_width + 1)
    doubled = jnp.concatenate([packed, packed], axis=0)
    start = (rows_total - row_y) % rows_total
    packed = lax.dynamic_slice_in_dim(doubled, start, rows_total, axis=0)
    returned = lax.all_to_all(packed, "sy", 0, 0, tiled=True)
    back_out, back_lse = unpack(returned)
    source_row = lax.broadcasted_iota(jnp.int32, back_lse.shape, 0)
    back_lse = jnp.where(source_row < row_y, back_lse, NEG_FILL)
    out2, lse2 = merge(
        [own_out2] + [back_out[i] for i in range(rows_total)],
        [own_lse2] + [back_lse[i] for i in range(rows_total)],
    )
    full_out, full_lse = spread_back(out2, lse2, chooser2)
    full_outs.append(full_out)
    full_lses.append(full_lse)

    lse_stack = jnp.stack(full_lses)
    level_top = jnp.max(lse_stack, axis=0)
    level_weights = jnp.exp(lse_stack - level_top[None])
    mixed_heads = (
        jnp.sum(level_weights[..., None] * jnp.stack(full_outs), axis=0)
        / jnp.sum(level_weights, axis=0)[..., None]
    )
    heads_out = mixed_heads.astype(jnp.bfloat16).reshape(row_count, head_count * head_width)
    chips = lax.axis_size("hx")
    cores = lax.axis_size("hc")
    copies = jnp.broadcast_to(heads_out[None], (chips,) + heads_out.shape)
    same_core = lax.all_to_all(copies, "hx", 0, 0, tiled=True)
    copies = jnp.broadcast_to(same_core[None], (cores,) + same_core.shape)
    gathered = lax.all_to_all(copies, "hc", 0, 0, tiled=True)
    weight = out_weight.reshape(chips, cores, head_count * head_width, out_weight.shape[1])
    projected = jnp.einsum(
        "cxtr,xcro->to", gathered, weight, preferred_element_type=jnp.float32
    )
    return projected.astype(jnp.bfloat16)


def solution(mesh):
    seq_count, head_count = mesh.devices.shape
    split = jax.sharding.Mesh(
        mesh.devices.reshape(seq_count // ROW, ROW, head_count // 2, 2), SEQ_AXES + HEAD_AXES
    )
    return jax.shard_map(
        local,
        mesh=split,
        in_specs=(
            P(SEQ_AXES, HEAD_AXES),
            P(SEQ_AXES, HEAD_AXES),
            P(SEQ_AXES, HEAD_AXES),
            P(None, HEAD_AXES),
            P(None, HEAD_AXES),
        ),
        out_specs=P(SEQ_AXES, HEAD_AXES),
        check_vma=False,
    )
```

```python
import jax
import jax.numpy as jnp
from jax import lax
from jax.sharding import PartitionSpec as P

RATE_MID = 8
RATE_TOP = 32
SEG_ROWS = 1024
ROW = 16
TOK_DEV = 256


NEG_FILL = -1e30


def pick_rows(states, chooser, spacing):
    row_count, head_count, head_width = states.shape
    grouped = states.reshape(row_count // spacing, spacing, head_count, head_width)
    return jnp.einsum("nrhd,rh->nhd", grouped, chooser, preferred_element_type=jnp.float32).astype(
        jnp.bfloat16
    )


def attend(query_rows, key_rows, value_rows, allowed, scale_factor):
    scores = (
        jnp.einsum("qhd,khd->hqk", query_rows, key_rows, preferred_element_type=jnp.float32)
        * scale_factor
    )
    if allowed is not None:
        scores = jnp.where(allowed[None], scores, NEG_FILL)
    highest = jnp.max(scores, axis=2, keepdims=True)
    weights = jnp.exp(scores - highest)
    totals = jnp.sum(weights, axis=2, keepdims=True)
    shares = (weights / totals).astype(jnp.bfloat16)
    result = jnp.einsum("hqk,khd->qhd", shares, value_rows, preferred_element_type=jnp.float32)
    return (result, (highest + jnp.log(totals))[:, :, 0].T)


def merge(outs, lses):
    lse_stack = jnp.stack(lses)
    top = jnp.max(lse_stack, axis=0)
    weights = jnp.exp(lse_stack - top[None])
    total = jnp.sum(weights, axis=0)
    out = jnp.sum(weights[..., None] * jnp.stack(outs), axis=0) / total[..., None]
    return out, top + jnp.log(total)


def spread_back(level_out, level_lse, chooser):
    picked = chooser.astype(jnp.float32)
    sparse_count, head_count, head_width = level_out.shape
    row_count = sparse_count * chooser.shape[0]
    full_out = (level_out[:, None, :, :] * picked[None, :, :, None]).reshape(
        row_count, head_count, head_width
    )
    full_lse = jnp.where(chooser[None], level_lse[:, None, :], NEG_FILL).reshape(
        row_count, head_count
    )
    return (full_out, full_lse)


def level_setup(query_all, key_all, value_all, offset_row, spacing):
    head_count = query_all.shape[1]
    chooser = (
        lax.broadcasted_iota(jnp.int32, (spacing, head_count), 0) == (offset_row % spacing)[None, :]
    )
    chooser_bf = chooser.astype(jnp.bfloat16)
    query_rows = pick_rows(query_all, chooser_bf, spacing)
    pair_rows = jnp.stack(
        [pick_rows(key_all, chooser_bf, spacing), pick_rows(value_all, chooser_bf, spacing)], axis=1
    )
    return (chooser, query_rows, pair_rows)


def pack(out, lse):
    return jnp.concatenate([out, lse[..., None]], axis=-1)


def unpack(packed):
    return packed[..., :-1], packed[..., -1]


SEQ_AXES = ("sy", "sz")
HEAD_AXES = ("hx", "hc")
ROW_AXES = "sz"


def split3(value):
    high = value.astype(jnp.bfloat16)
    rest = value - high.astype(jnp.float32)
    middle = rest.astype(jnp.bfloat16)
    low = (rest - middle.astype(jnp.float32)).astype(jnp.bfloat16)
    return jnp.stack([high, middle, low], axis=-1)


def join3(parts):
    parts = parts.astype(jnp.float32)
    return parts[..., 0] + parts[..., 1] + parts[..., 2]


def local(queries, key_states, value_states, level_offsets, out_weight):
    row_count = queries.shape[0]
    head_count = level_offsets.shape[1]
    head_width = queries.shape[1] // head_count
    scale_factor = head_width ** (-0.5)
    rows_total = lax.axis_size("sy")
    row_len = lax.axis_size("sz")
    seq_count = rows_total * row_len
    row_y = lax.axis_index("sy")
    row_z = lax.axis_index("sz")
    seq_index = row_y * row_len + row_z
    query_all = queries.reshape(row_count, head_count, head_width)
    key_all = key_states.reshape(row_count, head_count, head_width)
    value_all = value_states.reshape(row_count, head_count, head_width)
    full_outs = []
    full_lses = []

    span0 = SEG_ROWS // row_count
    chooser0, query0, pair0 = level_setup(query_all, key_all, value_all, level_offsets[0], 1)
    arrived = []
    for shift in range(span0 - 1, 0, -1):
        pairs = [(s, s + shift) for s in range(seq_count) if s % span0 + shift < span0]
        arrived.append(lax.ppermute(pair0, SEQ_AXES, pairs))
    buffer0 = jnp.concatenate(arrived + [pair0], axis=0)
    shape0 = (row_count, span0 * row_count)
    key_index = lax.broadcasted_iota(jnp.int32, shape0, 1)
    query_index = lax.broadcasted_iota(jnp.int32, shape0, 0)
    lowest = (span0 - 1 - seq_index % span0) * row_count
    allowed0 = (key_index >= lowest) & (key_index <= (span0 - 1) * row_count + query_index)
    out0, lse0 = attend(query0, buffer0[:, 0], buffer0[:, 1], allowed0, scale_factor)
    full_out, full_lse = spread_back(out0, lse0, chooser0)
    full_outs.append(full_out)
    full_lses.append(full_lse)

    chooser1, query1, pair1 = level_setup(query_all, key_all, value_all, level_offsets[1], RATE_MID)
    chooser2, query2, pair2 = level_setup(query_all, key_all, value_all, level_offsets[2], RATE_TOP)
    count1 = pair1.shape[0]
    count2 = pair2.shape[0]
    ring = lax.all_gather(jnp.concatenate([pair1, pair2], axis=0), ROW_AXES)
    row1 = ring[:, :count1]
    row2 = ring[:, count1:]

    def own_row(query_rows, row_blocks, count):
        keys = row_blocks.reshape(row_len * count, 2, head_count, head_width)
        shape = (count, row_len * count)
        key_index = lax.broadcasted_iota(jnp.int32, shape, 1)
        query_index = lax.broadcasted_iota(jnp.int32, shape, 0)
        source = key_index // count
        allowed = jnp.where(
            source == row_z, key_index % count <= query_index, source < row_z
        )
        return attend(query_rows, keys[:, 0], keys[:, 1], allowed, scale_factor)

    def whole_row(query_rows, row_blocks, count):
        keys = row_blocks.reshape(row_len * count, 2, head_count, head_width)
        return attend(query_rows, keys[:, 0], keys[:, 1], None, scale_factor)

    up = [(s, s - row_len) for s in range(seq_count) if (s // row_len) % 2 == 1]
    down = [(s, s + row_len) for s in range(seq_count) if (s // row_len) % 2 == 0]
    visiting1 = lax.ppermute(query1, SEQ_AXES, up)
    own_out1, own_lse1 = own_row(query1, row1, count1)
    cross1 = lax.ppermute(pack(*whole_row(visiting1, row1, count1)), SEQ_AXES, down)
    cross_out1, cross_lse1 = unpack(cross1)
    cross_lse1 = jnp.where(row_y % 2 == 1, cross_lse1, NEG_FILL)
    out1, lse1 = merge([own_out1, cross_out1], [own_lse1, cross_lse1])
    full_out, full_lse = spread_back(out1, lse1, chooser1)
    full_outs.append(full_out)
    full_lses.append(full_lse)

    own_out2, own_lse2 = own_row(query2, row2, count2)
    visiting = [query2]
    for gap in range(1, rows_total):
        pairs = [(s, s - gap * row_len) for s in range(seq_count) if s // row_len >= gap]
        visiting.append(lax.ppermute(query2, SEQ_AXES, pairs))
    cross_out, cross_lse = whole_row(jnp.concatenate(visiting, axis=0), row2, count2)
    packed = pack(cross_out, cross_lse).reshape(rows_total, count2, head_count, head_width + 1)
    doubled = jnp.concatenate([packed, packed], axis=0)
    start = (rows_total - row_y) % rows_total
    packed = lax.dynamic_slice_in_dim(doubled, start, rows_total, axis=0)
    returned = lax.all_to_all(packed, "sy", 0, 0, tiled=True)
    back_out, back_lse = unpack(returned)
    source_row = lax.broadcasted_iota(jnp.int32, back_lse.shape, 0)
    back_lse = jnp.where(source_row < row_y, back_lse, NEG_FILL)
    out2, lse2 = merge(
        [own_out2] + [back_out[i] for i in range(rows_total)],
        [own_lse2] + [back_lse[i] for i in range(rows_total)],
    )
    full_out, full_lse = spread_back(out2, lse2, chooser2)
    full_outs.append(full_out)
    full_lses.append(full_lse)

    lse_stack = jnp.stack(full_lses)
    level_top = jnp.max(lse_stack, axis=0)
    level_weights = jnp.exp(lse_stack - level_top[None])
    mixed_heads = (
        jnp.sum(level_weights[..., None] * jnp.stack(full_outs), axis=0)
        / jnp.sum(level_weights, axis=0)[..., None]
    )
    heads_out = mixed_heads.astype(jnp.bfloat16).reshape(row_count, head_count * head_width)
    chips = lax.axis_size("hx")
    cores = lax.axis_size("hc")
    copies = jnp.broadcast_to(heads_out[None], (chips,) + heads_out.shape)
    same_core = lax.all_to_all(copies, "hx", 0, 0, tiled=True)
    other_core = lax.ppermute(same_core, "hc", [(0, 1), (1, 0)])
    weight = out_weight.reshape(chips, cores, head_count * head_width, out_weight.shape[1])
    core = lax.axis_index("hc")
    mine = lax.dynamic_index_in_dim(weight, core, 1, keepdims=False)
    theirs = lax.dynamic_index_in_dim(weight, 1 - core, 1, keepdims=False)
    projected = jnp.einsum(
        "xtr,xro->to", same_core, mine, preferred_element_type=jnp.float32
    ) + jnp.einsum("xtr,xro->to", other_core, theirs, preferred_element_type=jnp.float32)
    return projected.astype(jnp.bfloat16)


def solution(mesh):
    seq_count, head_count = mesh.devices.shape
    split = jax.sharding.Mesh(
        mesh.devices.reshape(seq_count // ROW, ROW, head_count // 2, 2), SEQ_AXES + HEAD_AXES
    )
    return jax.shard_map(
        local,
        mesh=split,
        in_specs=(
            P(SEQ_AXES, HEAD_AXES),
            P(SEQ_AXES, HEAD_AXES),
            P(SEQ_AXES, HEAD_AXES),
            P(None, HEAD_AXES),
            P(None, HEAD_AXES),
        ),
        out_specs=P(SEQ_AXES, HEAD_AXES),
        check_vma=False,
    )
```

```python
import jax
import jax.numpy as jnp
from jax import lax
from jax.sharding import PartitionSpec as P

RATE_MID = 8
RATE_TOP = 32
SEG_ROWS = 1024
ROW = 16
TOK_DEV = 256


NEG_FILL = -1e30


def pick_rows(states, chooser, spacing):
    row_count, head_count, head_width = states.shape
    grouped = states.reshape(row_count // spacing, spacing, head_count, head_width)
    return jnp.einsum("nrhd,rh->nhd", grouped, chooser, preferred_element_type=jnp.float32).astype(
        jnp.bfloat16
    )


def attend(query_rows, key_rows, value_rows, allowed, scale_factor):
    scores = (
        jnp.einsum("qhd,khd->hqk", query_rows, key_rows, preferred_element_type=jnp.float32)
        * scale_factor
    )
    if allowed is not None:
        scores = jnp.where(allowed[None], scores, NEG_FILL)
    highest = jnp.max(scores, axis=2, keepdims=True)
    weights = jnp.exp(scores - highest)
    totals = jnp.sum(weights, axis=2, keepdims=True)
    shares = (weights / totals).astype(jnp.bfloat16)
    result = jnp.einsum("hqk,khd->qhd", shares, value_rows, preferred_element_type=jnp.float32)
    return (result, (highest + jnp.log(totals))[:, :, 0].T)


def merge(outs, lses):
    lse_stack = jnp.stack(lses)
    top = jnp.max(lse_stack, axis=0)
    weights = jnp.exp(lse_stack - top[None])
    total = jnp.sum(weights, axis=0)
    out = jnp.sum(weights[..., None] * jnp.stack(outs), axis=0) / total[..., None]
    return out, top + jnp.log(total)


def spread_back(level_out, level_lse, chooser):
    picked = chooser.astype(jnp.float32)
    sparse_count, head_count, head_width = level_out.shape
    row_count = sparse_count * chooser.shape[0]
    full_out = (level_out[:, None, :, :] * picked[None, :, :, None]).reshape(
        row_count, head_count, head_width
    )
    full_lse = jnp.where(chooser[None], level_lse[:, None, :], NEG_FILL).reshape(
        row_count, head_count
    )
    return (full_out, full_lse)


def level_setup(query_all, key_all, value_all, offset_row, spacing):
    head_count = query_all.shape[1]
    chooser = (
        lax.broadcasted_iota(jnp.int32, (spacing, head_count), 0) == (offset_row % spacing)[None, :]
    )
    chooser_bf = chooser.astype(jnp.bfloat16)
    query_rows = pick_rows(query_all, chooser_bf, spacing)
    pair_rows = jnp.stack(
        [pick_rows(key_all, chooser_bf, spacing), pick_rows(value_all, chooser_bf, spacing)], axis=1
    )
    return (chooser, query_rows, pair_rows)


def pack(out, lse):
    return jnp.concatenate([out, lse[..., None]], axis=-1)


def unpack(packed):
    return packed[..., :-1], packed[..., -1]


SEQ_AXES = ("sy", "sz")
HEAD_AXES = ("hx", "hc")
ROW_AXES = "sz"


def split3(value):
    high = value.astype(jnp.bfloat16)
    rest = value - high.astype(jnp.float32)
    middle = rest.astype(jnp.bfloat16)
    low = (rest - middle.astype(jnp.float32)).astype(jnp.bfloat16)
    return jnp.stack([high, middle, low], axis=-1)


def join3(parts):
    parts = parts.astype(jnp.float32)
    return parts[..., 0] + parts[..., 1] + parts[..., 2]


def local(queries, key_states, value_states, level_offsets, out_weight):
    row_count = queries.shape[0]
    head_count = level_offsets.shape[1]
    head_width = queries.shape[1] // head_count
    scale_factor = head_width ** (-0.5)
    rows_total = lax.axis_size("sy")
    row_len = lax.axis_size("sz")
    seq_count = rows_total * row_len
    row_y = lax.axis_index("sy")
    row_z = lax.axis_index("sz")
    seq_index = row_y * row_len + row_z
    query_all = queries.reshape(row_count, head_count, head_width)
    key_all = key_states.reshape(row_count, head_count, head_width)
    value_all = value_states.reshape(row_count, head_count, head_width)
    full_outs = []
    full_lses = []

    chooser1, query1, pair1 = level_setup(query_all, key_all, value_all, level_offsets[1], RATE_MID)
    chooser2, query2, pair2 = level_setup(query_all, key_all, value_all, level_offsets[2], RATE_TOP)
    count1 = pair1.shape[0]
    count2 = pair2.shape[0]
    copies = jnp.broadcast_to(query2[None], (rows_total,) + query2.shape)
    column_queries = lax.all_to_all(copies, "sy", 0, 0, tiled=True)
    payload, column_queries = lax.optimization_barrier(
        (jnp.concatenate([pair1, pair2], axis=0), column_queries)
    )
    ring = lax.all_gather(payload, ROW_AXES)

    span0 = SEG_ROWS // row_count
    chooser0, query0, pair0 = level_setup(query_all, key_all, value_all, level_offsets[0], 1)
    pair0, ring = lax.optimization_barrier((pair0, ring))
    arrived = []
    for shift in range(span0 - 1, 0, -1):
        pairs = [(s, s + shift) for s in range(seq_count) if s % span0 + shift < span0]
        arrived.append(lax.ppermute(pair0, SEQ_AXES, pairs))
    buffer0 = jnp.concatenate(arrived + [pair0], axis=0)
    shape0 = (row_count, span0 * row_count)
    key_index = lax.broadcasted_iota(jnp.int32, shape0, 1)
    query_index = lax.broadcasted_iota(jnp.int32, shape0, 0)
    lowest = (span0 - 1 - seq_index % span0) * row_count
    allowed0 = (key_index >= lowest) & (key_index <= (span0 - 1) * row_count + query_index)
    out0, lse0 = attend(query0, buffer0[:, 0], buffer0[:, 1], allowed0, scale_factor)
    full_out, full_lse = spread_back(out0, lse0, chooser0)
    full_outs.append(full_out)
    full_lses.append(full_lse)

    row1 = ring[:, :count1]
    row2 = ring[:, count1:]

    def own_row(query_rows, row_blocks, count):
        keys = row_blocks.reshape(row_len * count, 2, head_count, head_width)
        shape = (count, row_len * count)
        key_index = lax.broadcasted_iota(jnp.int32, shape, 1)
        query_index = lax.broadcasted_iota(jnp.int32, shape, 0)
        source = key_index // count
        allowed = jnp.where(
            source == row_z, key_index % count <= query_index, source < row_z
        )
        return attend(query_rows, keys[:, 0], keys[:, 1], allowed, scale_factor)

    def whole_row(query_rows, row_blocks, count):
        keys = row_blocks.reshape(row_len * count, 2, head_count, head_width)
        return attend(query_rows, keys[:, 0], keys[:, 1], None, scale_factor)

    up = [(s, s - row_len) for s in range(seq_count) if (s // row_len) % 2 == 1]
    down = [(s, s + row_len) for s in range(seq_count) if (s // row_len) % 2 == 0]
    visiting1 = lax.ppermute(query1, SEQ_AXES, up)
    own_out1, own_lse1 = own_row(query1, row1, count1)
    cross1 = lax.ppermute(pack(*whole_row(visiting1, row1, count1)), SEQ_AXES, down)
    cross_out1, cross_lse1 = unpack(cross1)
    cross_lse1 = jnp.where(row_y % 2 == 1, cross_lse1, NEG_FILL)
    out1, lse1 = merge([own_out1, cross_out1], [own_lse1, cross_lse1])
    full_out, full_lse = spread_back(out1, lse1, chooser1)
    full_outs.append(full_out)
    full_lses.append(full_lse)

    own_out2, own_lse2 = own_row(query2, row2, count2)
    cross_out, cross_lse = whole_row(
        column_queries.reshape(rows_total * count2, head_count, head_width), row2, count2
    )
    packed = pack(cross_out, cross_lse).reshape(rows_total, count2, head_count, head_width + 1)
    returned = lax.all_to_all(packed, "sy", 0, 0, tiled=True)
    back_out, back_lse = unpack(returned)
    source_row = lax.broadcasted_iota(jnp.int32, back_lse.shape, 0)
    back_lse = jnp.where(source_row < row_y, back_lse, NEG_FILL)
    out2, lse2 = merge(
        [own_out2] + [back_out[i] for i in range(rows_total)],
        [own_lse2] + [back_lse[i] for i in range(rows_total)],
    )
    full_out, full_lse = spread_back(out2, lse2, chooser2)
    full_outs.append(full_out)
    full_lses.append(full_lse)

    lse_stack = jnp.stack(full_lses)
    level_top = jnp.max(lse_stack, axis=0)
    level_weights = jnp.exp(lse_stack - level_top[None])
    mixed_heads = (
        jnp.sum(level_weights[..., None] * jnp.stack(full_outs), axis=0)
        / jnp.sum(level_weights, axis=0)[..., None]
    )
    heads_out = mixed_heads.astype(jnp.bfloat16).reshape(row_count, head_count * head_width)
    chips = lax.axis_size("hx")
    cores = lax.axis_size("hc")
    copies = jnp.broadcast_to(heads_out[None], (chips,) + heads_out.shape)
    same_core = lax.all_to_all(copies, "hx", 0, 0, tiled=True)
    other_core = lax.ppermute(same_core, "hc", [(0, 1), (1, 0)])
    weight = out_weight.reshape(chips, cores, head_count * head_width, out_weight.shape[1])
    core = lax.axis_index("hc")
    mine = lax.dynamic_index_in_dim(weight, core, 1, keepdims=False)
    theirs = lax.dynamic_index_in_dim(weight, 1 - core, 1, keepdims=False)
    projected = jnp.einsum(
        "xtr,xro->to", same_core, mine, preferred_element_type=jnp.float32
    ) + jnp.einsum("xtr,xro->to", other_core, theirs, preferred_element_type=jnp.float32)
    return projected.astype(jnp.bfloat16)


def solution(mesh):
    seq_count, head_count = mesh.devices.shape
    split = jax.sharding.Mesh(
        mesh.devices.reshape(seq_count // ROW, ROW, head_count // 2, 2), SEQ_AXES + HEAD_AXES
    )
    return jax.shard_map(
        local,
        mesh=split,
        in_specs=(
            P(SEQ_AXES, HEAD_AXES),
            P(SEQ_AXES, HEAD_AXES),
            P(SEQ_AXES, HEAD_AXES),
            P(None, HEAD_AXES),
            P(None, HEAD_AXES),
        ),
        out_specs=P(SEQ_AXES, HEAD_AXES),
        check_vma=False,
    )
```

```python
import jax
import jax.numpy as jnp
from jax import lax
from jax.sharding import PartitionSpec as P

RATE_MID = 8
RATE_TOP = 32
SEG_ROWS = 1024
ROW = 16
TOK_DEV = 256


NEG_FILL = -1e30


def pick_rows(states, chooser, spacing):
    row_count, head_count, head_width = states.shape
    grouped = states.reshape(row_count // spacing, spacing, head_count, head_width)
    return jnp.einsum("nrhd,rh->nhd", grouped, chooser, preferred_element_type=jnp.float32).astype(
        jnp.bfloat16
    )


def attend(query_rows, key_rows, value_rows, allowed, scale_factor):
    scores = (
        jnp.einsum("qhd,khd->hqk", query_rows, key_rows, preferred_element_type=jnp.float32)
        * scale_factor
    )
    if allowed is not None:
        scores = jnp.where(allowed[None], scores, NEG_FILL)
    highest = jnp.max(scores, axis=2, keepdims=True)
    weights = jnp.exp(scores - highest)
    totals = jnp.sum(weights, axis=2, keepdims=True)
    shares = (weights / totals).astype(jnp.bfloat16)
    result = jnp.einsum("hqk,khd->qhd", shares, value_rows, preferred_element_type=jnp.float32)
    return (result, (highest + jnp.log(totals))[:, :, 0].T)


def merge(outs, lses):
    lse_stack = jnp.stack(lses)
    top = jnp.max(lse_stack, axis=0)
    weights = jnp.exp(lse_stack - top[None])
    total = jnp.sum(weights, axis=0)
    out = jnp.sum(weights[..., None] * jnp.stack(outs), axis=0) / total[..., None]
    return out, top + jnp.log(total)


def spread_back(level_out, level_lse, chooser):
    picked = chooser.astype(jnp.float32)
    sparse_count, head_count, head_width = level_out.shape
    row_count = sparse_count * chooser.shape[0]
    full_out = (level_out[:, None, :, :] * picked[None, :, :, None]).reshape(
        row_count, head_count, head_width
    )
    full_lse = jnp.where(chooser[None], level_lse[:, None, :], NEG_FILL).reshape(
        row_count, head_count
    )
    return (full_out, full_lse)


def level_setup(query_all, key_all, value_all, offset_row, spacing):
    head_count = query_all.shape[1]
    chooser = (
        lax.broadcasted_iota(jnp.int32, (spacing, head_count), 0) == (offset_row % spacing)[None, :]
    )
    chooser_bf = chooser.astype(jnp.bfloat16)
    query_rows = pick_rows(query_all, chooser_bf, spacing)
    pair_rows = jnp.stack(
        [pick_rows(key_all, chooser_bf, spacing), pick_rows(value_all, chooser_bf, spacing)], axis=1
    )
    return (chooser, query_rows, pair_rows)


def pack(out, lse):
    return jnp.concatenate([out, lse[..., None]], axis=-1)


def unpack(packed):
    return packed[..., :-1], packed[..., -1]


SEQ_AXES = ("sy", "sz")
HEAD_AXES = ("hx", "hc")
ROW_AXES = "sz"


def split3(value):
    high = value.astype(jnp.bfloat16)
    rest = value - high.astype(jnp.float32)
    middle = rest.astype(jnp.bfloat16)
    low = (rest - middle.astype(jnp.float32)).astype(jnp.bfloat16)
    return jnp.stack([high, middle, low], axis=-1)


def join3(parts):
    parts = parts.astype(jnp.float32)
    return parts[..., 0] + parts[..., 1] + parts[..., 2]


def local(queries, key_states, value_states, level_offsets, out_weight):
    row_count = queries.shape[0]
    head_count = level_offsets.shape[1]
    head_width = queries.shape[1] // head_count
    scale_factor = head_width ** (-0.5)
    rows_total = lax.axis_size("sy")
    row_len = lax.axis_size("sz")
    seq_count = rows_total * row_len
    row_y = lax.axis_index("sy")
    row_z = lax.axis_index("sz")
    seq_index = row_y * row_len + row_z
    query_all = queries.reshape(row_count, head_count, head_width)
    key_all = key_states.reshape(row_count, head_count, head_width)
    value_all = value_states.reshape(row_count, head_count, head_width)
    full_outs = []
    full_lses = []

    chooser1, query1, pair1 = level_setup(query_all, key_all, value_all, level_offsets[1], RATE_MID)
    chooser2, query2, pair2 = level_setup(query_all, key_all, value_all, level_offsets[2], RATE_TOP)
    count1 = pair1.shape[0]
    count2 = pair2.shape[0]
    copies = jnp.broadcast_to(query2[None], (rows_total,) + query2.shape)
    column_queries = lax.all_to_all(copies, "sy", 0, 0, tiled=True)
    payload, column_queries = lax.optimization_barrier(
        (jnp.concatenate([pair1, pair2], axis=0), column_queries)
    )
    ring = lax.all_gather(payload, ROW_AXES)

    span0 = SEG_ROWS // row_count
    query_late, key_late, value_late, ring = lax.optimization_barrier(
        (query_all, key_all, value_all, ring)
    )
    chooser0, query0, pair0 = level_setup(query_late, key_late, value_late, level_offsets[0], 1)
    arrived = []
    for shift in range(span0 - 1, 0, -1):
        pairs = [(s, s + shift) for s in range(seq_count) if s % span0 + shift < span0]
        arrived.append(lax.ppermute(pair0, SEQ_AXES, pairs))
    buffer0 = jnp.concatenate(arrived + [pair0], axis=0)
    shape0 = (row_count, span0 * row_count)
    key_index = lax.broadcasted_iota(jnp.int32, shape0, 1)
    query_index = lax.broadcasted_iota(jnp.int32, shape0, 0)
    lowest = (span0 - 1 - seq_index % span0) * row_count
    allowed0 = (key_index >= lowest) & (key_index <= (span0 - 1) * row_count + query_index)
    out0, lse0 = attend(query0, buffer0[:, 0], buffer0[:, 1], allowed0, scale_factor)
    full_out, full_lse = spread_back(out0, lse0, chooser0)
    full_outs.append(full_out)
    full_lses.append(full_lse)

    row1 = ring[:, :count1]
    row2 = ring[:, count1:]

    def own_row(query_rows, row_blocks, count):
        keys = row_blocks.reshape(row_len * count, 2, head_count, head_width)
        shape = (count, row_len * count)
        key_index = lax.broadcasted_iota(jnp.int32, shape, 1)
        query_index = lax.broadcasted_iota(jnp.int32, shape, 0)
        source = key_index // count
        allowed = jnp.where(
            source == row_z, key_index % count <= query_index, source < row_z
        )
        return attend(query_rows, keys[:, 0], keys[:, 1], allowed, scale_factor)

    def whole_row(query_rows, row_blocks, count):
        keys = row_blocks.reshape(row_len * count, 2, head_count, head_width)
        return attend(query_rows, keys[:, 0], keys[:, 1], None, scale_factor)

    up = [(s, s - row_len) for s in range(seq_count) if (s // row_len) % 2 == 1]
    down = [(s, s + row_len) for s in range(seq_count) if (s // row_len) % 2 == 0]
    visiting1 = lax.ppermute(query1, SEQ_AXES, up)
    own_out1, own_lse1 = own_row(query1, row1, count1)
    cross1 = lax.ppermute(pack(*whole_row(visiting1, row1, count1)), SEQ_AXES, down)
    cross_out1, cross_lse1 = unpack(cross1)
    cross_lse1 = jnp.where(row_y % 2 == 1, cross_lse1, NEG_FILL)
    out1, lse1 = merge([own_out1, cross_out1], [own_lse1, cross_lse1])
    full_out, full_lse = spread_back(out1, lse1, chooser1)
    full_outs.append(full_out)
    full_lses.append(full_lse)

    own_out2, own_lse2 = own_row(query2, row2, count2)
    cross_out, cross_lse = whole_row(
        column_queries.reshape(rows_total * count2, head_count, head_width), row2, count2
    )
    packed = pack(cross_out, cross_lse).reshape(rows_total, count2, head_count, head_width + 1)
    returned = lax.all_to_all(packed, "sy", 0, 0, tiled=True)
    back_out, back_lse = unpack(returned)
    source_row = lax.broadcasted_iota(jnp.int32, back_lse.shape, 0)
    back_lse = jnp.where(source_row < row_y, back_lse, NEG_FILL)
    out2, lse2 = merge(
        [own_out2] + [back_out[i] for i in range(rows_total)],
        [own_lse2] + [back_lse[i] for i in range(rows_total)],
    )
    full_out, full_lse = spread_back(out2, lse2, chooser2)
    full_outs.append(full_out)
    full_lses.append(full_lse)

    lse_stack = jnp.stack(full_lses)
    level_top = jnp.max(lse_stack, axis=0)
    level_weights = jnp.exp(lse_stack - level_top[None])
    mixed_heads = (
        jnp.sum(level_weights[..., None] * jnp.stack(full_outs), axis=0)
        / jnp.sum(level_weights, axis=0)[..., None]
    )
    heads_out = mixed_heads.astype(jnp.bfloat16).reshape(row_count, head_count * head_width)
    chips = lax.axis_size("hx")
    cores = lax.axis_size("hc")
    copies = jnp.broadcast_to(heads_out[None], (chips,) + heads_out.shape)
    same_core = lax.all_to_all(copies, "hx", 0, 0, tiled=True)
    other_core = lax.ppermute(same_core, "hc", [(0, 1), (1, 0)])
    weight = out_weight.reshape(chips, cores, head_count * head_width, out_weight.shape[1])
    core = lax.axis_index("hc")
    mine = lax.dynamic_index_in_dim(weight, core, 1, keepdims=False)
    theirs = lax.dynamic_index_in_dim(weight, 1 - core, 1, keepdims=False)
    projected = jnp.einsum(
        "xtr,xro->to", same_core, mine, preferred_element_type=jnp.float32
    ) + jnp.einsum("xtr,xro->to", other_core, theirs, preferred_element_type=jnp.float32)
    return projected.astype(jnp.bfloat16)


def solution(mesh):
    seq_count, head_count = mesh.devices.shape
    split = jax.sharding.Mesh(
        mesh.devices.reshape(seq_count // ROW, ROW, head_count // 2, 2), SEQ_AXES + HEAD_AXES
    )
    return jax.shard_map(
        local,
        mesh=split,
        in_specs=(
            P(SEQ_AXES, HEAD_AXES),
            P(SEQ_AXES, HEAD_AXES),
            P(SEQ_AXES, HEAD_AXES),
            P(None, HEAD_AXES),
            P(None, HEAD_AXES),
        ),
        out_specs=P(SEQ_AXES, HEAD_AXES),
        check_vma=False,
    )
```
